32 devices in a mesh: grp: 2 (over y), row: 8 (over z, x), chan: 2 (over core).
Axes of the slice: x: 2, y: 2, z: 4, core: 2. Of those that a mesh axis runs over, the one named last changes fastest.
Arguments:
- band_strip: bfloat16 [424, 64, 128], P('chan', ('grp', 'row')), parts along dimension 1, may hold values from -6 to 6
- conv_weight: bfloat16 [1024, 9, 424], P('row', None, 'chan'), may hold values from -0.09375 to 0.09375
- gdn_gamma: bfloat16 [1024, 1024], P('chan'), as said below
- gdn_beta: float32 [1024], P('chan'), may hold values from 0.5 to 2
- cotangent: bfloat16 [1024, 64, 128], P('chan', ('grp', 'row')), parts along dimension 1, may hold values from -6 to 6
Outputs:
- latent: bfloat16 [1024, 64, 128], P('chan', ('grp', 'row')), parts along dimension 1
- grad_strip: float32 [424, 64, 128], P('chan', ('grp', 'row')), parts along dimension 1
- grad_gamma: float32 [2048, 1024], P(('grp', 'chan')), parts along dimension 0
- grad_beta: float32 [2048], P(('grp', 'chan')), parts along dimension 0
The draws below stay inside these ranges and needn't reach their ends.
There are 2 independent parts, one for each index of `grp`. The reference program is written for one: setup_inputs(seed, part) draws one part's arguments, and reference() takes and returns one part's arrays. A program takes and returns all parts, laid end to end along the dimension named above; an argument that names none is the same for every part. Nothing has to cross between parts.
Inputs may be any that keep to these rules, and one draw needn't show every extreme that they name: `gdn_gamma`: gamma's entries are non-negative.
All inputs are finite; a program needn't handle non-finite values.
Results may differ from the reference program's by a relative error of at most 0.0054.
Values may be sent and summed in bfloat16 or wider, within the bound.
No kernel may reach another device: no remote copies, remote signals or barrier semaphores. Data moves between devices by JAX's collectives and lax.ppermute only.
A program may use at most 64 MiB of HBM per device.

```python
import math
import jax
import jax.numpy as jnp
from jax import lax

C_IN = 424
C_LAT = 1024
W = 128
ROWS = 32
PIXELS = 4096


def draw_gdn_gamma(key, part):
    key_off = jax.random.fold_in(key, 11)
    key_diag = jax.random.fold_in(key, 12)
    exponent = jax.random.uniform(key_off, (C_LAT, C_LAT), jnp.float32, -4.6, 0.0)
    off_diag = jnp.exp(exponent) * (3.0 / C_LAT)
    diagonal = jnp.exp(jax.random.uniform(key_diag, (C_LAT,), jnp.float32, math.log(0.1), math.log(1.5)))
    identity = jnp.eye(C_LAT, dtype=jnp.float32)
    return (off_diag + identity * diagonal[:, None]).astype(jnp.bfloat16)


def block_scale(stream_key, shape, pieces, smallest, largest):
    factor_of, own = 1.0, jax.random.fold_in(stream_key, 6)
    for dim, parts in pieces:
        draws = jnp.exp(jax.random.uniform(jax.random.fold_in(own, dim), (parts,), jnp.float32, smallest / len(pieces), largest / len(pieces)))
        factor_of = factor_of * jnp.repeat(draws, shape[dim] // parts).reshape([-1 if axis == dim else 1 for axis in range(len(shape))])
    return factor_of


def gaussian(own_key, extent, spread, bound, pieces=(), kind=jnp.bfloat16):
    result = jax.random.normal(own_key, extent, jnp.float32) * spread
    if len(pieces) > 0:
        result = block_scale(own_key, extent, pieces, -0.22, 0.18) * result
    return jnp.clip(result, min=-bound, max=bound).astype(kind)


def setup_inputs(seed: int = 0, part: int = 0) -> dict:
    arg_keys = jax.random.split(jax.random.key(seed), 6)
    part_splits = jax.random.split(jax.random.fold_in(arg_keys[5], part), 6)
    return {
        "band_strip": gaussian(part_splits[0], (C_IN, ROWS, W), 1.0, 6.0, ((0, 2), (1, 8))),
        "conv_weight": gaussian(arg_keys[1], (C_LAT, 9, C_IN), (9 * C_IN) ** -0.5, 0.09375, ((0, 8), (2, 2))),
        "gdn_gamma": draw_gdn_gamma(jax.random.fold_in(arg_keys[5], 71), part),
        "gdn_beta": jnp.clip(jnp.exp(math.log(2.0) - 1.3862944 * jax.random.uniform(arg_keys[3], (C_LAT,), jnp.float32) ** block_scale(arg_keys[3], (C_LAT,), ((0, 2),), -0.2, 0.2)), 0.5, 2.0),
        "cotangent": gaussian(part_splits[4], (C_LAT, ROWS, W), 1.0, 6.0, ((0, 2), (1, 8))),
    }


TAPS = ((-1, -1), (-1, 0), (-1, 1), (0, -1), (0, 0), (0, 1), (1, -1), (1, 0), (1, 1))

def reference(band_strip, conv_weight, gdn_gamma, gdn_beta, cotangent):
    padded = jnp.pad(band_strip, ((0, 0), (1, 1), (1, 1)))
    pre = jnp.zeros((C_LAT, ROWS * W), jnp.float32)
    for tap_index, (row_shift, col_shift) in enumerate(TAPS):
        window = padded[:, 1 + row_shift:1 + row_shift + ROWS, 1 + col_shift:1 + col_shift + W].reshape(C_IN, ROWS * W)
        pre = pre + jnp.dot(conv_weight[:, tap_index, :], window, preferred_element_type=jnp.float32)
    squares = (pre * pre).astype(jnp.bfloat16)
    norm_value = gdn_beta[:, None] + jnp.dot(gdn_gamma, squares, preferred_element_type=jnp.float32)
    inverse = lax.rsqrt(norm_value)
    latent = (pre * inverse).astype(jnp.bfloat16)
    upstream = cotangent.reshape(C_LAT, ROWS * W).astype(jnp.float32)
    shares = (-0.5 * upstream * pre * inverse * inverse * inverse).astype(jnp.bfloat16)
    back_sum = jnp.dot(gdn_gamma.T, shares, preferred_element_type=jnp.float32)
    latent_grad = (upstream * inverse + 2.0 * pre * back_sum).astype(jnp.bfloat16)
    scale_factor = 1.0 / PIXELS ** 0.5
    grad_gamma = jnp.dot(shares, squares.T, preferred_element_type=jnp.float32) * scale_factor
    grad_beta = lax.optimization_barrier(jnp.sum(shares.astype(jnp.float32), axis=1)) * scale_factor
    grad_padded = jnp.pad(latent_grad.reshape(C_LAT, ROWS, W), ((0, 0), (1, 1), (1, 1)))
    grad_strip = jnp.zeros((C_IN, ROWS * W), jnp.float32)
    for tap_index, (row_shift, col_shift) in enumerate(TAPS):
        window = grad_padded[:, 1 - row_shift:1 - row_shift + ROWS, 1 - col_shift:1 - col_shift + W].reshape(C_LAT, ROWS * W)
        grad_strip = grad_strip + jnp.dot(conv_weight[:, tap_index, :].T, window, preferred_element_type=jnp.float32)
    return (latent.reshape(C_LAT, ROWS, W), grad_strip.reshape(C_IN, ROWS, W), grad_gamma, grad_beta)
```

```python
import math

import jax
import jax.numpy as jnp
from jax import lax
from jax.sharding import PartitionSpec as P

TAPS = ((-1, -1), (-1, 0), (-1, 1), (0, -1), (0, 0), (0, 1), (1, -1), (1, 0), (1, 1))
SWAP = [(0, 1), (1, 0)]


def extended(shard, sides, width):
    for axis, dim in sides:
        count, length = (lax.axis_size(axis), shard.shape[dim])
        up = [(i, (i + 1) % count) for i in range(count - 1)]
        down = [(j, i) for i, j in up]
        last = lax.slice_in_dim(shard, length - width, length, axis=dim)
        leading = lax.slice_in_dim(shard, 0, width, axis=dim)
        before = lax.ppermute(last, axis, up)
        after = lax.ppermute(leading, axis, down)
        shard = jnp.concatenate([before, shard, after], axis=dim)
    return shard


def tap_columns(rimmed, row_count, col_count):
    padded = jnp.pad(rimmed, ((0, 0), (0, 0), (1, 1)))
    stacked = jnp.stack(
        [
            padded[
                :,
                1 + row_shift : 1 + row_shift + row_count,
                1 + col_shift : 1 + col_shift + col_count,
            ]
            for row_shift, col_shift in TAPS
        ],
        axis=0,
    )
    return stacked.reshape(9 * rimmed.shape[0], row_count * col_count)


def chan_gather(x):
    other = lax.ppermute(x, "chan", SWAP)
    first = lax.axis_index("chan") == 0
    return jnp.where(first, jnp.concatenate([x, other], 0), jnp.concatenate([other, x], 0))


def chan_scatter_sum(x):
    half = x.shape[0] // 2
    first = lax.axis_index("chan") == 0
    top, bottom = x[:half], x[half:]
    mine = jnp.where(first, top, bottom)
    theirs = jnp.where(first, bottom, top)
    return mine + lax.ppermute(theirs, "chan", SWAP)


def ring_order(mesh):
    count = mesh.shape["row"]
    try:
        coords = [tuple(d.coords) for d in mesh.devices[0, :, 0]]
    except Exception:
        return list(range(count))
    xs = sorted({c[0] for c in coords})
    zs = sorted({c[2] for c in coords})
    if len(xs) * len(zs) != count or len(zs) % 2:
        return list(range(count))
    where = {(c[0], c[2]): i for i, c in enumerate(coords)}
    path = [where[(xs[0], zs[0])]]
    for k, z in enumerate(zs):
        cols = xs[1:] if k % 2 == 0 else xs[:0:-1]
        path += [where[(x, z)] for x in cols]
    path += [where[(xs[0], z)] for z in zs[:0:-1]]
    return path if len(set(path)) == count else list(range(count))


def ring_sum(blocks, ring):
    count = len(ring)
    forward = [(ring[i], ring[(i + 1) % count]) for i in range(count)]
    backward = [(b, a) for a, b in forward]
    position = jnp.asarray([ring.index(i) for i in range(count)], jnp.int32)[lax.axis_index("row")]

    def chunks(x, part):
        half = x.shape[0] // 2
        piece = x[part * half : (part + 1) * half]
        return piece.reshape((count, half // count) + x.shape[1:])

    split = [[chunks(x, part) for x in blocks] for part in range(2)]
    moves = (forward, backward)
    signs = (1, -1)

    def pick(part, step):
        index = (position - signs[part] * (1 + step)) % count
        return [jnp.take(c, index, axis=0) for c in split[part]]

    carry = [pick(part, 0) for part in range(2)]
    for step in range(1, count):
        for part in range(2):
            got = lax.ppermute(carry[part], "row", moves[part])
            carry[part] = [g + o for g, o in zip(got, pick(part, step))]
    gathered = [[c] for c in carry]
    for step in range(1, count):
        for part in range(2):
            gathered[part].append(lax.ppermute(gathered[part][-1], "row", moves[part]))
    results = []
    for leaf in range(len(blocks)):
        halves = []
        for part in range(2):
            stacked = jnp.stack([g[leaf] for g in gathered[part]], 0)
            order = (signs[part] * (position - jnp.arange(count))) % count
            halves.append(jnp.take(stacked, order, axis=0).reshape((-1,) + stacked.shape[2:]))
        results.append(jnp.concatenate(halves, 0))
    return results


def make_per_device(ring):
    def per_device(band_strip, conv_weight, gdn_gamma, gdn_beta, cotangent):
        in_local = band_strip.shape[0]
        row_count = band_strip.shape[1]
        col_count = band_strip.shape[2]
        pixels = row_count * col_count
        lat_local = gdn_gamma.shape[0]
        first = lax.axis_index("chan") == 0
        rimmed = extended(band_strip, (("row", 1),), 1)
        columns = tap_columns(rimmed, row_count, col_count)
        shard_piece = lax.all_gather(conv_weight, "row", axis=0, tiled=True)
        flat = shard_piece.reshape(shard_piece.shape[0], 9 * in_local)
        partial_value = jnp.dot(flat, columns, preferred_element_type=jnp.float32)
        pre = chan_scatter_sum(partial_value)
        squares_own = (pre * pre).astype(jnp.bfloat16)
        squares = chan_gather(squares_own)
        norm_value = gdn_beta[:, None] + jnp.dot(gdn_gamma, squares, preferred_element_type=jnp.float32)
        inverse = lax.rsqrt(norm_value)
        latent = (pre * inverse).astype(jnp.bfloat16)
        upstream = cotangent.reshape(lat_local, pixels).astype(jnp.float32)
        shares = (-0.5 * upstream * pre * inverse * inverse * inverse).astype(jnp.bfloat16)
        gamma_left, gamma_right = gdn_gamma[:, :lat_local], gdn_gamma[:, lat_local:]
        gamma_mine = jnp.where(first, gamma_left, gamma_right)
        gamma_theirs = lax.ppermute(jnp.where(first, gamma_right, gamma_left), "chan", SWAP)
        gamma_cols = jnp.where(
            first,
            jnp.concatenate([gamma_mine, gamma_theirs], 0),
            jnp.concatenate([gamma_theirs, gamma_mine], 0),
        )
        shares_all = chan_gather(shares)
        back_sum = lax.dot_general(
            gamma_cols, shares_all, (((0,), (0,)), ((), ())), preferred_element_type=jnp.float32
        )
        latent_grad = (upstream * inverse + 2.0 * pre * back_sum).astype(jnp.bfloat16)
        gamma_terms = lax.dot_general(
            shares, squares, (((1,), (1,)), ((), ())), preferred_element_type=jnp.float32
        )
        beta_terms = jnp.sum(shares.astype(jnp.float32), axis=1)
        if len(ring) <= 16:
            gamma_total, beta_total = ring_sum([gamma_terms, beta_terms], ring)
        else:
            gamma_total, beta_total = lax.psum((gamma_terms, beta_terms), "row")
        scale_factor = 1.0 / math.sqrt(pixels * lax.axis_size("row"))
        grad_gamma = gamma_total * scale_factor
        grad_beta = beta_total * scale_factor
        grad_all = chan_gather(latent_grad.reshape(lat_local, row_count, col_count))
        grad_rimmed = extended(grad_all, (("row", 1),), 1)
        grad_padded = jnp.pad(grad_rimmed, ((0, 0), (0, 0), (1, 1)))
        running = jnp.zeros((in_local, pixels), jnp.float32)
        count_rows = shard_piece.shape[0]
        for tap_index, (row_shift, col_shift) in enumerate(TAPS):
            window = grad_padded[
                :, 1 - row_shift : 1 - row_shift + row_count, 1 - col_shift : 1 - col_shift + col_count
            ].reshape(count_rows, pixels)
            running = running + lax.dot_general(
                shard_piece[:, tap_index, :],
                window,
                (((0,), (0,)), ((), ())),
                preferred_element_type=jnp.float32,
            )
        return (
            latent.reshape(lat_local, row_count, col_count),
            running.reshape(in_local, row_count, col_count),
            grad_gamma,
            grad_beta,
        )

    return per_device


def solution(mesh):
    return jax.shard_map(
        make_per_device(ring_order(mesh)),
        mesh=mesh,
        in_specs=(
            P("chan", ("grp", "row"), None),
            P("row", None, "chan"),
            P("chan", None),
            P("chan"),
            P("chan", ("grp", "row"), None),
        ),
        out_specs=(
            P("chan", ("grp", "row"), None),
            P("chan", ("grp", "row"), None),
            P(("grp", "chan"), None),
            P(("grp", "chan")),
        ),
        check_vma=False,
    )
```

```python
import math

import jax
import jax.numpy as jnp
from jax import lax
from jax.sharding import PartitionSpec as P

TAPS = ((-1, -1), (-1, 0), (-1, 1), (0, -1), (0, 0), (0, 1), (1, -1), (1, 0), (1, 1))
SWAP = [(0, 1), (1, 0)]


def extended(shard, sides, width):
    for axis, dim in sides:
        count, length = (lax.axis_size(axis), shard.shape[dim])
        up = [(i, (i + 1) % count) for i in range(count - 1)]
        down = [(j, i) for i, j in up]
        last = lax.slice_in_dim(shard, length - width, length, axis=dim)
        leading = lax.slice_in_dim(shard, 0, width, axis=dim)
        before = lax.ppermute(last, axis, up)
        after = lax.ppermute(leading, axis, down)
        shard = jnp.concatenate([before, shard, after], axis=dim)
    return shard


def tap_columns(rimmed, row_count, col_count):
    padded = jnp.pad(rimmed, ((0, 0), (0, 0), (1, 1)))
    stacked = jnp.stack(
        [
            padded[
                :,
                1 + row_shift : 1 + row_shift + row_count,
                1 + col_shift : 1 + col_shift + col_count,
            ]
            for row_shift, col_shift in TAPS
        ],
        axis=0,
    )
    return stacked.reshape(9 * rimmed.shape[0], row_count * col_count)


def chan_gather(x):
    other = lax.ppermute(x, "chan", SWAP)
    both = jnp.concatenate([x, other], 0)
    return jnp.roll(both, lax.axis_index("chan") * x.shape[0], axis=0)


def chan_gather_into(mine, other):
    both = jnp.concatenate([mine, other], 0)
    return jnp.roll(both, lax.axis_index("chan") * mine.shape[0], axis=0)


def chan_scatter_sum(x):
    half = x.shape[0] // 2
    index = lax.axis_index("chan")
    mine = lax.dynamic_slice_in_dim(x, index * half, half, 0)
    theirs = lax.dynamic_slice_in_dim(x, (1 - index) * half, half, 0)
    return mine + lax.ppermute(theirs, "chan", SWAP)


def ring_order(mesh):
    count = mesh.shape["row"]
    try:
        coords = [tuple(d.coords) for d in mesh.devices[0, :, 0]]
    except Exception:
        return list(range(count))
    xs = sorted({c[0] for c in coords})
    zs = sorted({c[2] for c in coords})
    if len(xs) * len(zs) != count or len(zs) % 2:
        return list(range(count))
    where = {(c[0], c[2]): i for i, c in enumerate(coords)}
    path = [where[(xs[0], zs[0])]]
    for k, z in enumerate(zs):
        cols = xs[1:] if k % 2 == 0 else xs[:0:-1]
        path += [where[(x, z)] for x in cols]
    path += [where[(xs[0], z)] for z in zs[:0:-1]]
    return path if len(set(path)) == count else list(range(count))


def ring_sum(blocks, ring):
    count = len(ring)
    forward = [(ring[i], ring[(i + 1) % count]) for i in range(count)]
    backward = [(b, a) for a, b in forward]
    position = jnp.asarray([ring.index(i) for i in range(count)], jnp.int32)[lax.axis_index("row")]

    def chunks(x, part):
        half = x.shape[0] // 2
        piece = x[part * half : (part + 1) * half]
        return piece.reshape((count, half // count) + x.shape[1:])

    split = [[chunks(x, part) for x in blocks] for part in range(2)]
    moves = (forward, backward)
    signs = (1, -1)

    def pick(part, step):
        index = (position - signs[part] * (1 + step)) % count
        return [jnp.take(c, index, axis=0) for c in split[part]]

    carry = [pick(part, 0) for part in range(2)]
    for step in range(1, count):
        for part in range(2):
            got = lax.ppermute(carry[part], "row", moves[part])
            carry[part] = [g + o for g, o in zip(got, pick(part, step))]
    gathered = [[c] for c in carry]
    for step in range(1, count):
        for part in range(2):
            gathered[part].append(lax.ppermute(gathered[part][-1], "row", moves[part]))
    results = []
    for leaf in range(len(blocks)):
        halves = []
        for part in range(2):
            stacked = jnp.stack([g[leaf] for g in gathered[part]], 0)
            order = (signs[part] * (position - jnp.arange(count))) % count
            halves.append(jnp.take(stacked, order, axis=0).reshape((-1,) + stacked.shape[2:]))
        results.append(jnp.concatenate(halves, 0))
    return results


def make_per_device(ring):
    def per_device(band_strip, conv_weight, gdn_gamma, gdn_beta, cotangent):
        in_local = band_strip.shape[0]
        row_count = band_strip.shape[1]
        col_count = band_strip.shape[2]
        pixels = row_count * col_count
        lat_local = gdn_gamma.shape[0]
        rimmed = extended(band_strip, (("row", 1),), 1)
        columns = tap_columns(rimmed, row_count, col_count)
        shard_piece = lax.all_gather(conv_weight, "row", axis=0, tiled=True)
        flat = shard_piece.reshape(shard_piece.shape[0], 9 * in_local)
        partial_value = jnp.dot(flat, columns, preferred_element_type=jnp.float32)
        pre = chan_scatter_sum(partial_value)
        squares_own = (pre * pre).astype(jnp.bfloat16)
        squares = chan_gather(squares_own)
        norm_value = gdn_beta[:, None] + jnp.dot(gdn_gamma, squares, preferred_element_type=jnp.float32)
        inverse = lax.rsqrt(norm_value)
        latent = (pre * inverse).astype(jnp.bfloat16)
        upstream = cotangent.reshape(lat_local, pixels).astype(jnp.float32)
        shares = (-0.5 * upstream * pre * inverse * inverse * inverse).astype(jnp.bfloat16)
        index = lax.axis_index("chan")
        gamma_mine = lax.dynamic_slice_in_dim(gdn_gamma, index * lat_local, lat_local, 1)
        gamma_theirs = lax.dynamic_slice_in_dim(gdn_gamma, (1 - index) * lat_local, lat_local, 1)
        gamma_cols = chan_gather_into(gamma_mine, lax.ppermute(gamma_theirs, "chan", SWAP))
        shares_all = chan_gather(shares)
        back_sum = lax.dot_general(
            gamma_cols, shares_all, (((0,), (0,)), ((), ())), preferred_element_type=jnp.float32
        )
        latent_grad = (upstream * inverse + 2.0 * pre * back_sum).astype(jnp.bfloat16)
        gamma_terms = lax.dot_general(
            shares, squares, (((1,), (1,)), ((), ())), preferred_element_type=jnp.float32
        )
        beta_terms = jnp.sum(shares.astype(jnp.float32), axis=1)
        joined = jnp.concatenate(
            [gamma_terms, jnp.broadcast_to(beta_terms[:, None], (lat_local, 128))], 1
        )
        if len(ring) <= 16:
            (joined_total,) = ring_sum([joined], ring)
        else:
            joined_total = lax.psum(joined, "row")
        gamma_total = joined_total[:, : gamma_terms.shape[1]]
        beta_total = joined_total[:, gamma_terms.shape[1]]
        scale_factor = 1.0 / math.sqrt(pixels * lax.axis_size("row"))
        grad_gamma = gamma_total * scale_factor
        grad_beta = beta_total * scale_factor
        grad_all = chan_gather(latent_grad.reshape(lat_local, row_count, col_count))
        grad_rimmed = extended(grad_all, (("row", 1),), 1)
        grad_padded = jnp.pad(grad_rimmed, ((0, 0), (0, 0), (1, 1)))
        running = jnp.zeros((in_local, pixels), jnp.float32)
        count_rows = shard_piece.shape[0]
        for tap_index, (row_shift, col_shift) in enumerate(TAPS):
            window = grad_padded[
                :, 1 - row_shift : 1 - row_shift + row_count, 1 - col_shift : 1 - col_shift + col_count
            ].reshape(count_rows, pixels)
            running = running + lax.dot_general(
                shard_piece[:, tap_index, :],
                window,
                (((0,), (0,)), ((), ())),
                preferred_element_type=jnp.float32,
            )
        return (
            latent.reshape(lat_local, row_count, col_count),
            running.reshape(in_local, row_count, col_count),
            grad_gamma,
            grad_beta,
        )

    return per_device


def solution(mesh):
    return jax.shard_map(
        make_per_device(ring_order(mesh)),
        mesh=mesh,
        in_specs=(
            P("chan", ("grp", "row"), None),
            P("row", None, "chan"),
            P("chan", None),
            P("chan"),
            P("chan", ("grp", "row"), None),
        ),
        out_specs=(
            P("chan", ("grp", "row"), None),
            P("chan", ("grp", "row"), None),
            P(("grp", "chan"), None),
            P(("grp", "chan")),
        ),
        check_vma=False,
    )
```

```python
import math

import jax
import jax.numpy as jnp
from jax import lax
from jax.sharding import PartitionSpec as P

TAPS = ((-1, -1), (-1, 0), (-1, 1), (0, -1), (0, 0), (0, 1), (1, -1), (1, 0), (1, 1))
SWAP = [(0, 1), (1, 0)]


def extended(shard, sides, width):
    for axis, dim in sides:
        count, length = (lax.axis_size(axis), shard.shape[dim])
        up = [(i, (i + 1) % count) for i in range(count - 1)]
        down = [(j, i) for i, j in up]
        last = lax.slice_in_dim(shard, length - width, length, axis=dim)
        leading = lax.slice_in_dim(shard, 0, width, axis=dim)
        before = lax.ppermute(last, axis, up)
        after = lax.ppermute(leading, axis, down)
        shard = jnp.concatenate([before, shard, after], axis=dim)
    return shard


def chan_gather(x):
    other = lax.ppermute(x, "chan", SWAP)
    both = jnp.concatenate([x, other], 0)
    return jnp.roll(both, lax.axis_index("chan") * x.shape[0], axis=0)


def chan_gather_into(mine, other):
    both = jnp.concatenate([mine, other], 0)
    return jnp.roll(both, lax.axis_index("chan") * mine.shape[0], axis=0)


def chan_scatter_sum(x):
    half = x.shape[0] // 2
    index = lax.axis_index("chan")
    mine = lax.dynamic_slice_in_dim(x, index * half, half, 0)
    theirs = lax.dynamic_slice_in_dim(x, (1 - index) * half, half, 0)
    return mine + lax.ppermute(theirs, "chan", SWAP)


def ring_order(mesh):
    count = mesh.shape["row"]
    try:
        coords = [tuple(d.coords) for d in mesh.devices[0, :, 0]]
    except Exception:
        return list(range(count))
    xs = sorted({c[0] for c in coords})
    zs = sorted({c[2] for c in coords})
    if len(xs) * len(zs) != count or len(zs) % 2:
        return list(range(count))
    where = {(c[0], c[2]): i for i, c in enumerate(coords)}
    path = [where[(xs[0], zs[0])]]
    for k, z in enumerate(zs):
        cols = xs[1:] if k % 2 == 0 else xs[:0:-1]
        path += [where[(x, z)] for x in cols]
    path += [where[(xs[0], z)] for z in zs[:0:-1]]
    return path if len(set(path)) == count else list(range(count))


def ring_sum(blocks, ring):
    count = len(ring)
    forward = [(ring[i], ring[(i + 1) % count]) for i in range(count)]
    backward = [(b, a) for a, b in forward]
    position = jnp.asarray([ring.index(i) for i in range(count)], jnp.int32)[lax.axis_index("row")]

    def chunks(x, part):
        half = x.shape[0] // 2
        piece = x[part * half : (part + 1) * half]
        return piece.reshape((count, half // count) + x.shape[1:])

    split = [[chunks(x, part) for x in blocks] for part in range(2)]
    moves = (forward, backward)
    signs = (1, -1)

    def pick(part, step):
        index = (position - signs[part] * (1 + step)) % count
        return [jnp.take(c, index, axis=0) for c in split[part]]

    carry = [pick(part, 0) for part in range(2)]
    for step in range(1, count):
        for part in range(2):
            got = lax.ppermute(carry[part], "row", moves[part])
            carry[part] = [g + o for g, o in zip(got, pick(part, step))]
    gathered = [[c] for c in carry]
    for step in range(1, count):
        for part in range(2):
            gathered[part].append(lax.ppermute(gathered[part][-1], "row", moves[part]))
    results = []
    for leaf in range(len(blocks)):
        halves = []
        for part in range(2):
            stacked = jnp.stack([g[leaf] for g in gathered[part]], 0)
            order = (signs[part] * (position - jnp.arange(count))) % count
            halves.append(jnp.take(stacked, order, axis=0).reshape((-1,) + stacked.shape[2:]))
        results.append(jnp.concatenate(halves, 0))
    return results


def make_per_device(ring):
    def per_device(band_strip, conv_weight, gdn_gamma, gdn_beta, cotangent):
        in_local = band_strip.shape[0]
        row_count = band_strip.shape[1]
        col_count = band_strip.shape[2]
        pixels = row_count * col_count
        lat_local = gdn_gamma.shape[0]
        rimmed = extended(band_strip, (("row", 1),), 1)
        strip_padded = jnp.pad(rimmed, ((0, 0), (0, 0), (1, 1)))
        shard_piece = lax.all_gather(conv_weight, "row", axis=0, tiled=True)
        partial_value = jnp.zeros((shard_piece.shape[0], pixels), jnp.float32)
        for tap_index, (row_shift, col_shift) in enumerate(TAPS):
            window = strip_padded[
                :, 1 + row_shift : 1 + row_shift + row_count, 1 + col_shift : 1 + col_shift + col_count
            ].reshape(in_local, pixels)
            partial_value = partial_value + jnp.dot(
                shard_piece[:, tap_index, :], window, preferred_element_type=jnp.float32
            )
        pre = chan_scatter_sum(partial_value)
        squares_own = (pre * pre).astype(jnp.bfloat16)
        squares = chan_gather(squares_own)
        norm_value = gdn_beta[:, None] + jnp.dot(gdn_gamma, squares, preferred_element_type=jnp.float32)
        inverse = lax.rsqrt(norm_value)
        latent = (pre * inverse).astype(jnp.bfloat16)
        upstream = cotangent.reshape(lat_local, pixels).astype(jnp.float32)
        shares = (-0.5 * upstream * pre * inverse * inverse * inverse).astype(jnp.bfloat16)
        index = lax.axis_index("chan")
        gamma_mine = lax.dynamic_slice_in_dim(gdn_gamma, index * lat_local, lat_local, 1)
        gamma_theirs = lax.dynamic_slice_in_dim(gdn_gamma, (1 - index) * lat_local, lat_local, 1)
        gamma_cols = chan_gather_into(gamma_mine, lax.ppermute(gamma_theirs, "chan", SWAP))
        shares_all = chan_gather(shares)
        back_sum = lax.dot_general(
            gamma_cols, shares_all, (((0,), (0,)), ((), ())), preferred_element_type=jnp.float32
        )
        latent_grad = (upstream * inverse + 2.0 * pre * back_sum).astype(jnp.bfloat16)
        gamma_terms = lax.dot_general(
            shares, squares, (((1,), (1,)), ((), ())), preferred_element_type=jnp.float32
        )
        beta_terms = jnp.sum(shares.astype(jnp.float32), axis=1)
        joined = jnp.concatenate(
            [gamma_terms, jnp.broadcast_to(beta_terms[:, None], (lat_local, 128))], 1
        )
        if len(ring) <= 16:
            (joined_total,) = ring_sum([joined], ring)
        else:
            joined_total = lax.psum(joined, "row")
        gamma_total = joined_total[:, : gamma_terms.shape[1]]
        beta_total = joined_total[:, gamma_terms.shape[1]]
        scale_factor = 1.0 / math.sqrt(pixels * lax.axis_size("row"))
        grad_gamma = gamma_total * scale_factor
        grad_beta = beta_total * scale_factor
        grad_all = chan_gather(latent_grad.reshape(lat_local, row_count, col_count))
        grad_rimmed = extended(grad_all, (("row", 1),), 1)
        grad_padded = jnp.pad(grad_rimmed, ((0, 0), (0, 0), (1, 1)))
        running = jnp.zeros((in_local, pixels), jnp.float32)
        count_rows = shard_piece.shape[0]
        for tap_index, (row_shift, col_shift) in enumerate(TAPS):
            window = grad_padded[
                :, 1 - row_shift : 1 - row_shift + row_count, 1 - col_shift : 1 - col_shift + col_count
            ].reshape(count_rows, pixels)
            running = running + lax.dot_general(
                shard_piece[:, tap_index, :],
                window,
                (((0,), (0,)), ((), ())),
                preferred_element_type=jnp.float32,
            )
        return (
            latent.reshape(lat_local, row_count, col_count),
            running.reshape(in_local, row_count, col_count),
            grad_gamma,
            grad_beta,
        )

    return per_device


def solution(mesh):
    return jax.shard_map(
        make_per_device(ring_order(mesh)),
        mesh=mesh,
        in_specs=(
            P("chan", ("grp", "row"), None),
            P("row", None, "chan"),
            P("chan", None),
            P("chan"),
            P("chan", ("grp", "row"), None),
        ),
        out_specs=(
            P("chan", ("grp", "row"), None),
            P("chan", ("grp", "row"), None),
            P(("grp", "chan"), None),
            P(("grp", "chan")),
        ),
        check_vma=False,
    )
```

```python
import math

import jax
import jax.numpy as jnp
from jax import lax
from jax.sharding import PartitionSpec as P

TAPS = ((-1, -1), (-1, 0), (-1, 1), (0, -1), (0, 0), (0, 1), (1, -1), (1, 0), (1, 1))
SWAP = [(0, 1), (1, 0)]


def extended(shard, sides, width):
    for axis, dim in sides:
        count, length = (lax.axis_size(axis), shard.shape[dim])
        up = [(i, (i + 1) % count) for i in range(count - 1)]
        down = [(j, i) for i, j in up]
        last = lax.slice_in_dim(shard, length - width, length, axis=dim)
        leading = lax.slice_in_dim(shard, 0, width, axis=dim)
        before = lax.ppermute(last, axis, up)
        after = lax.ppermute(leading, axis, down)
        shard = jnp.concatenate([before, shard, after], axis=dim)
    return shard


def chan_gather(x):
    other = lax.ppermute(x, "chan", SWAP)
    both = jnp.concatenate([x, other], 0)
    return jnp.roll(both, lax.axis_index("chan") * x.shape[0], axis=0)


def chan_gather_into(mine, other):
    both = jnp.concatenate([mine, other], 0)
    return jnp.roll(both, lax.axis_index("chan") * mine.shape[0], axis=0)


def chan_scatter_sum(x):
    half = x.shape[0] // 2
    index = lax.axis_index("chan")
    mine = lax.dynamic_slice_in_dim(x, index * half, half, 0)
    theirs = lax.dynamic_slice_in_dim(x, (1 - index) * half, half, 0)
    return mine + lax.ppermute(theirs, "chan", SWAP)


def ring_order(mesh):
    count = mesh.shape["row"]
    try:
        coords = [tuple(d.coords) for d in mesh.devices[0, :, 0]]
    except Exception:
        return list(range(count))
    xs = sorted({c[0] for c in coords})
    zs = sorted({c[2] for c in coords})
    if len(xs) * len(zs) != count or len(zs) % 2:
        return list(range(count))
    where = {(c[0], c[2]): i for i, c in enumerate(coords)}
    path = [where[(xs[0], zs[0])]]
    for k, z in enumerate(zs):
        cols = xs[1:] if k % 2 == 0 else xs[:0:-1]
        path += [where[(x, z)] for x in cols]
    path += [where[(xs[0], z)] for z in zs[:0:-1]]
    return path if len(set(path)) == count else list(range(count))


def ring_sum(blocks, ring):
    count = len(ring)
    forward = [(ring[i], ring[(i + 1) % count]) for i in range(count)]
    backward = [(b, a) for a, b in forward]
    position = jnp.asarray([ring.index(i) for i in range(count)], jnp.int32)[lax.axis_index("row")]

    def chunks(x, part):
        half = x.shape[0] // 2
        piece = x[part * half : (part + 1) * half]
        return piece.reshape((count, half // count) + x.shape[1:])

    split = [[chunks(x, part) for x in blocks] for part in range(2)]
    moves = (forward, backward)
    signs = (1, -1)

    def pick(part, step):
        index = (position - signs[part] * (1 + step)) % count
        return [jnp.take(c, index, axis=0) for c in split[part]]

    carry = [pick(part, 0) for part in range(2)]
    for step in range(1, count):
        for part in range(2):
            got = lax.ppermute(carry[part], "row", moves[part])
            carry[part] = [g + o for g, o in zip(got, pick(part, step))]
    gathered = [[c.astype(jnp.bfloat16) for c in part] for part in carry]
    gathered = [[c] for c in gathered]
    for step in range(1, count):
        for part in range(2):
            gathered[part].append(lax.ppermute(gathered[part][-1], "row", moves[part]))
    results = []
    for leaf in range(len(blocks)):
        halves = []
        for part in range(2):
            stacked = jnp.stack([g[leaf] for g in gathered[part]], 0)
            order = (signs[part] * (position - jnp.arange(count))) % count
            halves.append(jnp.take(stacked, order, axis=0).reshape((-1,) + stacked.shape[2:]))
        results.append(jnp.concatenate(halves, 0).astype(jnp.float32))
    return results


def make_per_device(ring):
    def per_device(band_strip, conv_weight, gdn_gamma, gdn_beta, cotangent):
        in_local = band_strip.shape[0]
        row_count = band_strip.shape[1]
        col_count = band_strip.shape[2]
        pixels = row_count * col_count
        lat_local = gdn_gamma.shape[0]
        rimmed = extended(band_strip, (("row", 1),), 1)
        strip_padded = jnp.pad(rimmed, ((0, 0), (0, 0), (1, 1)))
        shard_piece = lax.all_gather(conv_weight, "row", axis=0, tiled=True)
        partial_value = jnp.zeros((shard_piece.shape[0], pixels), jnp.float32)
        for tap_index, (row_shift, col_shift) in enumerate(TAPS):
            window = strip_padded[
                :, 1 + row_shift : 1 + row_shift + row_count, 1 + col_shift : 1 + col_shift + col_count
            ].reshape(in_local, pixels)
            partial_value = partial_value + jnp.dot(
                shard_piece[:, tap_index, :], window, preferred_element_type=jnp.float32
            )
        pre = chan_scatter_sum(partial_value)
        squares_own = (pre * pre).astype(jnp.bfloat16)
        squares = chan_gather(squares_own)
        norm_value = gdn_beta[:, None] + jnp.dot(gdn_gamma, squares, preferred_element_type=jnp.float32)
        inverse = lax.rsqrt(norm_value)
        latent = (pre * inverse).astype(jnp.bfloat16)
        upstream = cotangent.reshape(lat_local, pixels).astype(jnp.float32)
        shares = (-0.5 * upstream * pre * inverse * inverse * inverse).astype(jnp.bfloat16)
        index = lax.axis_index("chan")
        gamma_mine = lax.dynamic_slice_in_dim(gdn_gamma, index * lat_local, lat_local, 1)
        gamma_theirs = lax.dynamic_slice_in_dim(gdn_gamma, (1 - index) * lat_local, lat_local, 1)
        gamma_cols = chan_gather_into(gamma_mine, lax.ppermute(gamma_theirs, "chan", SWAP))
        shares_all = chan_gather(shares)
        back_sum = lax.dot_general(
            gamma_cols, shares_all, (((0,), (0,)), ((), ())), preferred_element_type=jnp.float32
        )
        latent_grad = (upstream * inverse + 2.0 * pre * back_sum).astype(jnp.bfloat16)
        gamma_terms = lax.dot_general(
            shares, squares, (((1,), (1,)), ((), ())), preferred_element_type=jnp.float32
        )
        beta_terms = jnp.sum(shares.astype(jnp.float32), axis=1)
        joined = jnp.concatenate(
            [gamma_terms, jnp.broadcast_to(beta_terms[:, None], (lat_local, 128))], 1
        )
        if len(ring) <= 16:
            (joined_total,) = ring_sum([joined], ring)
        else:
            joined_total = lax.psum(joined, "row")
        gamma_total = joined_total[:, : gamma_terms.shape[1]]
        beta_total = joined_total[:, gamma_terms.shape[1]]
        scale_factor = 1.0 / math.sqrt(pixels * lax.axis_size("row"))
        grad_gamma = gamma_total * scale_factor
        grad_beta = beta_total * scale_factor
        grad_all = chan_gather(latent_grad.reshape(lat_local, row_count, col_count))
        grad_rimmed = extended(grad_all, (("row", 1),), 1)
        grad_padded = jnp.pad(grad_rimmed, ((0, 0), (0, 0), (1, 1)))
        running = jnp.zeros((in_local, pixels), jnp.float32)
        count_rows = shard_piece.shape[0]
        for tap_index, (row_shift, col_shift) in enumerate(TAPS):
            window = grad_padded[
                :, 1 - row_shift : 1 - row_shift + row_count, 1 - col_shift : 1 - col_shift + col_count
            ].reshape(count_rows, pixels)
            running = running + lax.dot_general(
                shard_piece[:, tap_index, :],
                window,
                (((0,), (0,)), ((), ())),
                preferred_element_type=jnp.float32,
            )
        return (
            latent.reshape(lat_local, row_count, col_count),
            running.reshape(in_local, row_count, col_count),
            grad_gamma,
            grad_beta,
        )

    return per_device


def solution(mesh):
    return jax.shard_map(
        make_per_device(ring_order(mesh)),
        mesh=mesh,
        in_specs=(
            P("chan", ("grp", "row"), None),
            P("row", None, "chan"),
            P("chan", None),
            P("chan"),
            P("chan", ("grp", "row"), None),
        ),
        out_specs=(
            P("chan", ("grp", "row"), None),
            P("chan", ("grp", "row"), None),
            P(("grp", "chan"), None),
            P(("grp", "chan")),
        ),
        check_vma=False,
    )
```

```python
import math

import jax
import jax.numpy as jnp
from jax import lax
from jax.sharding import PartitionSpec as P

TAPS = ((-1, -1), (-1, 0), (-1, 1), (0, -1), (0, 0), (0, 1), (1, -1), (1, 0), (1, 1))
SWAP = [(0, 1), (1, 0)]


def extended(shard, sides, width):
    for axis, dim in sides:
        count, length = (lax.axis_size(axis), shard.shape[dim])
        up = [(i, (i + 1) % count) for i in range(count - 1)]
        down = [(j, i) for i, j in up]
        last = lax.slice_in_dim(shard, length - width, length, axis=dim)
        leading = lax.slice_in_dim(shard, 0, width, axis=dim)
        before = lax.ppermute(last, axis, up)
        after = lax.ppermute(leading, axis, down)
        shard = jnp.concatenate([before, shard, after], axis=dim)
    return shard


def chan_gather(x):
    other = lax.ppermute(x, "chan", SWAP)
    both = jnp.concatenate([x, other], 0)
    return jnp.roll(both, lax.axis_index("chan") * x.shape[0], axis=0)


def chan_gather_into(mine, other):
    both = jnp.concatenate([mine, other], 0)
    return jnp.roll(both, lax.axis_index("chan") * mine.shape[0], axis=0)


def chan_scatter_sum(x):
    half = x.shape[0] // 2
    index = lax.axis_index("chan")
    mine = lax.dynamic_slice_in_dim(x, index * half, half, 0)
    theirs = lax.dynamic_slice_in_dim(x, (1 - index) * half, half, 0)
    return mine + lax.ppermute(theirs, "chan", SWAP)


def ring_order(mesh):
    count = mesh.shape["row"]
    try:
        coords = [tuple(d.coords) for d in mesh.devices[0, :, 0]]
    except Exception:
        return list(range(count))
    xs = sorted({c[0] for c in coords})
    zs = sorted({c[2] for c in coords})
    if len(xs) * len(zs) != count or len(zs) % 2:
        return list(range(count))
    where = {(c[0], c[2]): i for i, c in enumerate(coords)}
    path = [where[(xs[0], zs[0])]]
    for k, z in enumerate(zs):
        cols = xs[1:] if k % 2 == 0 else xs[:0:-1]
        path += [where[(x, z)] for x in cols]
    path += [where[(xs[0], z)] for z in zs[:0:-1]]
    return path if len(set(path)) == count else list(range(count))


def ring_sum(blocks, ring):
    count = len(ring)
    forward = [(ring[i], ring[(i + 1) % count]) for i in range(count)]
    backward = [(b, a) for a, b in forward]
    position = jnp.asarray([ring.index(i) for i in range(count)], jnp.int32)[lax.axis_index("row")]

    def chunks(x, part):
        half = x.shape[0] // 2
        piece = x[part * half : (part + 1) * half]
        return piece.reshape((count, half // count) + x.shape[1:])

    split = [[chunks(x, part) for x in blocks] for part in range(2)]
    moves = (forward, backward)
    signs = (1, -1)

    def pick(part, step):
        index = (position - signs[part] * (1 + step)) % count
        return [jnp.take(c, index, axis=0) for c in split[part]]

    carry = [pick(part, 0) for part in range(2)]
    for step in range(1, count):
        for part in range(2):
            got = lax.ppermute(carry[part], "row", moves[part])
            carry[part] = [g + o for g, o in zip(got, pick(part, step))]
    gathered = [[c.astype(jnp.bfloat16) for c in part] for part in carry]
    gathered = [[c] for c in gathered]
    for step in range(1, count):
        for part in range(2):
            gathered[part].append(lax.ppermute(gathered[part][-1], "row", moves[part]))
    results = []
    for leaf in range(len(blocks)):
        halves = []
        for part in range(2):
            stacked = jnp.stack([g[leaf] for g in gathered[part]], 0)
            order = (signs[part] * (position - jnp.arange(count))) % count
            halves.append(jnp.take(stacked, order, axis=0).reshape((-1,) + stacked.shape[2:]))
        results.append(jnp.concatenate(halves, 0).astype(jnp.float32))
    return results


def make_per_device(ring):
    def per_device(band_strip, conv_weight, gdn_gamma, gdn_beta, cotangent):
        in_local = band_strip.shape[0]
        row_count = band_strip.shape[1]
        col_count = band_strip.shape[2]
        pixels = row_count * col_count
        lat_local = gdn_gamma.shape[0]
        rimmed = extended(band_strip, (("row", 1),), 1)
        strip_padded = jnp.pad(rimmed, ((0, 0), (0, 0), (1, 1)))
        shard_piece = lax.all_gather(conv_weight, "row", axis=0, tiled=True)
        partial_value = jnp.zeros((shard_piece.shape[0], pixels), jnp.float32)
        for tap_index, (row_shift, col_shift) in enumerate(TAPS):
            window = strip_padded[
                :, 1 + row_shift : 1 + row_shift + row_count, 1 + col_shift : 1 + col_shift + col_count
            ].reshape(in_local, pixels)
            partial_value = partial_value + jnp.dot(
                shard_piece[:, tap_index, :], window, preferred_element_type=jnp.float32
            )
        pre = lax.psum_scatter(partial_value, "chan", scatter_dimension=0, tiled=True)
        squares_own = (pre * pre).astype(jnp.bfloat16)
        squares = chan_gather(squares_own)
        norm_value = gdn_beta[:, None] + jnp.dot(gdn_gamma, squares, preferred_element_type=jnp.float32)
        inverse = lax.rsqrt(norm_value)
        latent = (pre * inverse).astype(jnp.bfloat16)
        upstream = cotangent.reshape(lat_local, pixels).astype(jnp.float32)
        shares = (-0.5 * upstream * pre * inverse * inverse * inverse).astype(jnp.bfloat16)
        index = lax.axis_index("chan")
        gamma_mine = lax.dynamic_slice_in_dim(gdn_gamma, index * lat_local, lat_local, 1)
        gamma_theirs = lax.dynamic_slice_in_dim(gdn_gamma, (1 - index) * lat_local, lat_local, 1)
        gamma_cols = chan_gather_into(gamma_mine, lax.ppermute(gamma_theirs, "chan", SWAP))
        shares_all = chan_gather(shares)
        back_sum = lax.dot_general(
            gamma_cols, shares_all, (((0,), (0,)), ((), ())), preferred_element_type=jnp.float32
        )
        latent_grad = (upstream * inverse + 2.0 * pre * back_sum).astype(jnp.bfloat16)
        gamma_terms = lax.dot_general(
            shares, squares, (((1,), (1,)), ((), ())), preferred_element_type=jnp.float32
        )
        beta_terms = jnp.sum(shares.astype(jnp.float32), axis=1)
        joined = jnp.concatenate(
            [gamma_terms, jnp.broadcast_to(beta_terms[:, None], (lat_local, 128))], 1
        )
        if len(ring) <= 16:
            (joined_total,) = ring_sum([joined], ring)
        else:
            joined_total = lax.psum(joined, "row")
        gamma_total = joined_total[:, : gamma_terms.shape[1]]
        beta_total = joined_total[:, gamma_terms.shape[1]]
        scale_factor = 1.0 / math.sqrt(pixels * lax.axis_size("row"))
        grad_gamma = gamma_total * scale_factor
        grad_beta = beta_total * scale_factor
        grad_all = chan_gather(latent_grad.reshape(lat_local, row_count, col_count))
        grad_rimmed = extended(grad_all, (("row", 1),), 1)
        grad_padded = jnp.pad(grad_rimmed, ((0, 0), (0, 0), (1, 1)))
        running = jnp.zeros((in_local, pixels), jnp.float32)
        count_rows = shard_piece.shape[0]
        for tap_index, (row_shift, col_shift) in enumerate(TAPS):
            window = grad_padded[
                :, 1 - row_shift : 1 - row_shift + row_count, 1 - col_shift : 1 - col_shift + col_count
            ].reshape(count_rows, pixels)
            running = running + lax.dot_general(
                shard_piece[:, tap_index, :],
                window,
                (((0,), (0,)), ((), ())),
                preferred_element_type=jnp.float32,
            )
        return (
            latent.reshape(lat_local, row_count, col_count),
            running.reshape(in_local, row_count, col_count),
            grad_gamma,
            grad_beta,
        )

    return per_device


def solution(mesh):
    return jax.shard_map(
        make_per_device(ring_order(mesh)),
        mesh=mesh,
        in_specs=(
            P("chan", ("grp", "row"), None),
            P("row", None, "chan"),
            P("chan", None),
            P("chan"),
            P("chan", ("grp", "row"), None),
        ),
        out_specs=(
            P("chan", ("grp", "row"), None),
            P("chan", ("grp", "row"), None),
            P(("grp", "chan"), None),
            P(("grp", "chan")),
        ),
        check_vma=False,
    )
```

```python
import math

import jax
import jax.numpy as jnp
from jax import lax
from jax.sharding import PartitionSpec as P

TAPS = ((-1, -1), (-1, 0), (-1, 1), (0, -1), (0, 0), (0, 1), (1, -1), (1, 0), (1, 1))
SWAP = [(0, 1), (1, 0)]


def extended(shard, sides, width):
    for axis, dim in sides:
        count, length = (lax.axis_size(axis), shard.shape[dim])
        up = [(i, (i + 1) % count) for i in range(count - 1)]
        down = [(j, i) for i, j in up]
        last = lax.slice_in_dim(shard, length - width, length, axis=dim)
        leading = lax.slice_in_dim(shard, 0, width, axis=dim)
        before = lax.ppermute(last, axis, up)
        after = lax.ppermute(leading, axis, down)
        shard = jnp.concatenate([before, shard, after], axis=dim)
    return shard


def chan_gather(x):
    other = lax.ppermute(x, "chan", SWAP)
    both = jnp.concatenate([x, other], 0)
    return jnp.roll(both, lax.axis_index("chan") * x.shape[0], axis=0)


def chan_gather_into(mine, other):
    both = jnp.concatenate([mine, other], 0)
    return jnp.roll(both, lax.axis_index("chan") * mine.shape[0], axis=0)


def chan_scatter_sum(x):
    half = x.shape[0] // 2
    index = lax.axis_index("chan")
    mine = lax.dynamic_slice_in_dim(x, index * half, half, 0)
    theirs = lax.dynamic_slice_in_dim(x, (1 - index) * half, half, 0)
    return mine + lax.ppermute(theirs, "chan", SWAP)


def ring_order(mesh):
    count = mesh.shape["row"]
    try:
        coords = [tuple(d.coords) for d in mesh.devices[0, :, 0]]
    except Exception:
        return list(range(count))
    xs = sorted({c[0] for c in coords})
    zs = sorted({c[2] for c in coords})
    if len(xs) * len(zs) != count or len(zs) % 2:
        return list(range(count))
    where = {(c[0], c[2]): i for i, c in enumerate(coords)}
    path = [where[(xs[0], zs[0])]]
    for k, z in enumerate(zs):
        cols = xs[1:] if k % 2 == 0 else xs[:0:-1]
        path += [where[(x, z)] for x in cols]
    path += [where[(xs[0], z)] for z in zs[:0:-1]]
    return path if len(set(path)) == count else list(range(count))


def ring_sum(blocks, ring):
    count = len(ring)
    forward = [(ring[i], ring[(i + 1) % count]) for i in range(count)]
    backward = [(b, a) for a, b in forward]
    position = jnp.asarray([ring.index(i) for i in range(count)], jnp.int32)[lax.axis_index("row")]

    def chunks(x, part):
        half = x.shape[0] // 2
        piece = x[part * half : (part + 1) * half]
        return piece.reshape((count, half // count) + x.shape[1:])

    split = [[chunks(x, part) for x in blocks] for part in range(2)]
    moves = (forward, backward)
    signs = (1, -1)

    def pick(part, step):
        index = (position - signs[part] * (1 + step)) % count
        return [jnp.take(c, index, axis=0) for c in split[part]]

    carry = [pick(part, 0) for part in range(2)]
    for step in range(1, count):
        for part in range(2):
            got = lax.ppermute(carry[part], "row", moves[part])
            carry[part] = [g + o for g, o in zip(got, pick(part, step))]
    gathered = [[c.astype(jnp.bfloat16) for c in part] for part in carry]
    gathered = [[c] for c in gathered]
    for step in range(1, count):
        for part in range(2):
            gathered[part].append(lax.ppermute(gathered[part][-1], "row", moves[part]))
    results = []
    for leaf in range(len(blocks)):
        halves = []
        for part in range(2):
            stacked = jnp.stack([g[leaf] for g in gathered[part]], 0)
            order = (signs[part] * (position - jnp.arange(count))) % count
            halves.append(jnp.take(stacked, order, axis=0).reshape((-1,) + stacked.shape[2:]))
        results.append(jnp.concatenate(halves, 0).astype(jnp.float32))
    return results


def make_per_device(ring):
    def per_device(band_strip, conv_weight, gdn_gamma, gdn_beta, cotangent):
        in_local = band_strip.shape[0]
        row_count = band_strip.shape[1]
        col_count = band_strip.shape[2]
        pixels = row_count * col_count
        lat_local = gdn_gamma.shape[0]
        rimmed = extended(band_strip, (("row", 1),), 1)
        strip_padded = jnp.pad(rimmed, ((0, 0), (0, 0), (1, 1)))
        shard_piece = lax.all_gather(conv_weight, "row", axis=0, tiled=True)
        partial_value = jnp.zeros((shard_piece.shape[0], pixels), jnp.float32)
        for tap_index, (row_shift, col_shift) in enumerate(TAPS):
            window = strip_padded[
                :, 1 + row_shift : 1 + row_shift + row_count, 1 + col_shift : 1 + col_shift + col_count
            ].reshape(in_local, pixels)
            partial_value = partial_value + jnp.dot(
                shard_piece[:, tap_index, :], window, preferred_element_type=jnp.float32
            )
        pre = lax.psum_scatter(partial_value, "chan", scatter_dimension=0, tiled=True)
        squares_own = (pre * pre).astype(jnp.bfloat16)
        squares = chan_gather(squares_own)
        norm_value = gdn_beta[:, None] + jnp.dot(gdn_gamma, squares, preferred_element_type=jnp.float32)
        inverse = lax.rsqrt(norm_value)
        latent = (pre * inverse).astype(jnp.bfloat16)
        upstream = cotangent.reshape(lat_local, pixels).astype(jnp.float32)
        shares = (-0.5 * upstream * pre * inverse * inverse * inverse).astype(jnp.bfloat16)
        index = lax.axis_index("chan")
        gamma_mine = lax.dynamic_slice_in_dim(gdn_gamma, index * lat_local, lat_local, 1)
        gamma_theirs = lax.dynamic_slice_in_dim(gdn_gamma, (1 - index) * lat_local, lat_local, 1)
        gamma_cols = chan_gather_into(gamma_mine, lax.ppermute(gamma_theirs, "chan", SWAP))
        shares_all = chan_gather(shares)
        back_sum = lax.dot_general(
            gamma_cols, shares_all, (((0,), (0,)), ((), ())), preferred_element_type=jnp.float32
        )
        latent_grad = (upstream * inverse + 2.0 * pre * back_sum).astype(jnp.bfloat16)
        gamma_terms = lax.dot_general(
            shares, squares, (((1,), (1,)), ((), ())), preferred_element_type=jnp.float32
        )
        beta_terms = jnp.sum(shares.astype(jnp.float32), axis=1)
        beta_wide = jnp.broadcast_to(beta_terms[None, :], (32, lat_local))
        beta_total = lax.psum(beta_wide, "row")[0]
        if len(ring) <= 16:
            (gamma_total,) = ring_sum([gamma_terms], ring)
        else:
            gamma_total = lax.psum(gamma_terms, "row")
        scale_factor = 1.0 / math.sqrt(pixels * lax.axis_size("row"))
        grad_gamma = gamma_total * scale_factor
        grad_beta = beta_total * scale_factor
        grad_all = chan_gather(latent_grad.reshape(lat_local, row_count, col_count))
        grad_rimmed = extended(grad_all, (("row", 1),), 1)
        grad_padded = jnp.pad(grad_rimmed, ((0, 0), (0, 0), (1, 1)))
        running = jnp.zeros((in_local, pixels), jnp.float32)
        count_rows = shard_piece.shape[0]
        for tap_index, (row_shift, col_shift) in enumerate(TAPS):
            window = grad_padded[
                :, 1 - row_shift : 1 - row_shift + row_count, 1 - col_shift : 1 - col_shift + col_count
            ].reshape(count_rows, pixels)
            running = running + lax.dot_general(
                shard_piece[:, tap_index, :],
                window,
                (((0,), (0,)), ((), ())),
                preferred_element_type=jnp.float32,
            )
        return (
            latent.reshape(lat_local, row_count, col_count),
            running.reshape(in_local, row_count, col_count),
            grad_gamma,
            grad_beta,
        )

    return per_device


def solution(mesh):
    return jax.shard_map(
        make_per_device(ring_order(mesh)),
        mesh=mesh,
        in_specs=(
            P("chan", ("grp", "row"), None),
            P("row", None, "chan"),
            P("chan", None),
            P("chan"),
            P("chan", ("grp", "row"), None),
        ),
        out_specs=(
            P("chan", ("grp", "row"), None),
            P("chan", ("grp", "row"), None),
            P(("grp", "chan"), None),
            P(("grp", "chan")),
        ),
        check_vma=False,
    )
```

```python
import math

import jax
import jax.numpy as jnp
from jax import lax
from jax.sharding import PartitionSpec as P

TAPS = ((-1, -1), (-1, 0), (-1, 1), (0, -1), (0, 0), (0, 1), (1, -1), (1, 0), (1, 1))
SWAP = [(0, 1), (1, 0)]


def extended(shard, sides, width):
    for axis, dim in sides:
        count, length = (lax.axis_size(axis), shard.shape[dim])
        up = [(i, (i + 1) % count) for i in range(count - 1)]
        down = [(j, i) for i, j in up]
        last = lax.slice_in_dim(shard, length - width, length, axis=dim)
        leading = lax.slice_in_dim(shard, 0, width, axis=dim)
        before = lax.ppermute(last, axis, up)
        after = lax.ppermute(leading, axis, down)
        shard = jnp.concatenate([before, shard, after], axis=dim)
    return shard


def chan_gather(x):
    other = lax.ppermute(x, "chan", SWAP)
    both = jnp.concatenate([x, other], 0)
    return jnp.roll(both, lax.axis_index("chan") * x.shape[0], axis=0)


def chan_gather_into(mine, other):
    both = jnp.concatenate([mine, other], 0)
    return jnp.roll(both, lax.axis_index("chan") * mine.shape[0], axis=0)


def chan_scatter_sum(x):
    half = x.shape[0] // 2
    index = lax.axis_index("chan")
    mine = lax.dynamic_slice_in_dim(x, index * half, half, 0)
    theirs = lax.dynamic_slice_in_dim(x, (1 - index) * half, half, 0)
    return mine + lax.ppermute(theirs, "chan", SWAP)


def ring_order(mesh):
    count = mesh.shape["row"]
    try:
        coords = [tuple(d.coords) for d in mesh.devices[0, :, 0]]
    except Exception:
        return list(range(count))
    xs = sorted({c[0] for c in coords})
    zs = sorted({c[2] for c in coords})
    if len(xs) * len(zs) != count or len(zs) % 2:
        return list(range(count))
    where = {(c[0], c[2]): i for i, c in enumerate(coords)}
    path = [where[(xs[0], zs[0])]]
    for k, z in enumerate(zs):
        cols = xs[1:] if k % 2 == 0 else xs[:0:-1]
        path += [where[(x, z)] for x in cols]
    path += [where[(xs[0], z)] for z in zs[:0:-1]]
    return path if len(set(path)) == count else list(range(count))


def ring_sum(blocks, ring):
    count = len(ring)
    forward = [(ring[i], ring[(i + 1) % count]) for i in range(count)]
    backward = [(b, a) for a, b in forward]
    position = jnp.asarray([ring.index(i) for i in range(count)], jnp.int32)[lax.axis_index("row")]

    def chunks(x, part):
        half = x.shape[0] // 2
        piece = x[part * half : (part + 1) * half]
        return piece.reshape((count, half // count) + x.shape[1:])

    split = [[chunks(x, part) for x in blocks] for part in range(2)]
    moves = (forward, backward)
    signs = (1, -1)

    def pick(part, step):
        index = (position - signs[part] * (1 + step)) % count
        return [jnp.take(c, index, axis=0) for c in split[part]]

    carry = [pick(part, 0) for part in range(2)]
    for step in range(1, count):
        for part in range(2):
            got = lax.ppermute(carry[part], "row", moves[part])
            carry[part] = [g + o for g, o in zip(got, pick(part, step))]
    gathered = [[c.astype(jnp.bfloat16) for c in part] for part in carry]
    gathered = [[c] for c in gathered]
    for step in range(1, count):
        for part in range(2):
            gathered[part].append(lax.ppermute(gathered[part][-1], "row", moves[part]))
    results = []
    for leaf in range(len(blocks)):
        halves = []
        for part in range(2):
            stacked = jnp.stack([g[leaf] for g in gathered[part]], 0)
            order = (signs[part] * (position - jnp.arange(count))) % count
            halves.append(jnp.take(stacked, order, axis=0).reshape((-1,) + stacked.shape[2:]))
        results.append(jnp.concatenate(halves, 0).astype(jnp.float32))
    return results


def make_per_device(ring):
    def per_device(band_strip, conv_weight, gdn_gamma, gdn_beta, cotangent):
        in_local = band_strip.shape[0]
        row_count = band_strip.shape[1]
        col_count = band_strip.shape[2]
        pixels = row_count * col_count
        lat_local = gdn_gamma.shape[0]
        rimmed = extended(band_strip, (("row", 1),), 1)
        strip_padded = jnp.pad(rimmed, ((0, 0), (0, 0), (1, 1)))
        shard_piece = lax.all_gather(conv_weight, "row", axis=0, tiled=True)
        partial_value = jnp.zeros((shard_piece.shape[0], pixels), jnp.float32)
        for tap_index, (row_shift, col_shift) in enumerate(TAPS):
            window = strip_padded[
                :, 1 + row_shift : 1 + row_shift + row_count, 1 + col_shift : 1 + col_shift + col_count
            ].reshape(in_local, pixels)
            partial_value = partial_value + jnp.dot(
                shard_piece[:, tap_index, :], window, preferred_element_type=jnp.float32
            )
        pre = lax.psum_scatter(partial_value, "chan", scatter_dimension=0, tiled=True)
        squares_own = (pre * pre).astype(jnp.bfloat16)
        squares = chan_gather(squares_own)
        norm_value = gdn_beta[:, None] + jnp.dot(gdn_gamma, squares, preferred_element_type=jnp.float32)
        inverse = lax.rsqrt(norm_value)
        latent = (pre * inverse).astype(jnp.bfloat16)
        upstream = cotangent.reshape(lat_local, pixels).astype(jnp.float32)
        shares = (-0.5 * upstream * pre * inverse * inverse * inverse).astype(jnp.bfloat16)
        index = lax.axis_index("chan")
        gamma_mine = lax.dynamic_slice_in_dim(gdn_gamma, index * lat_local, lat_local, 1)
        gamma_theirs = lax.dynamic_slice_in_dim(gdn_gamma, (1 - index) * lat_local, lat_local, 1)
        gamma_cols = chan_gather_into(gamma_mine, lax.ppermute(gamma_theirs, "chan", SWAP))
        shares_all = chan_gather(shares)
        back_sum = lax.dot_general(
            gamma_cols, shares_all, (((0,), (0,)), ((), ())), preferred_element_type=jnp.float32
        )
        latent_grad = (upstream * inverse + 2.0 * pre * back_sum).astype(jnp.bfloat16)
        lat_all = squares.shape[0]
        squares_ones = jnp.concatenate([squares, jnp.ones((128, pixels), squares.dtype)], 0)
        joined = lax.dot_general(
            shares, squares_ones, (((1,), (1,)), ((), ())), preferred_element_type=jnp.float32
        )
        if len(ring) <= 16:
            (joined_total,) = ring_sum([joined], ring)
        else:
            joined_total = lax.psum(joined, "row")
        gamma_total = joined_total[:, :lat_all]
        beta_total = joined_total[:, lat_all]
        scale_factor = 1.0 / math.sqrt(pixels * lax.axis_size("row"))
        grad_gamma = gamma_total * scale_factor
        grad_beta = beta_total * scale_factor
        grad_all = chan_gather(latent_grad.reshape(lat_local, row_count, col_count))
        grad_rimmed = extended(grad_all, (("row", 1),), 1)
        grad_padded = jnp.pad(grad_rimmed, ((0, 0), (0, 0), (1, 1)))
        running = jnp.zeros((in_local, pixels), jnp.float32)
        count_rows = shard_piece.shape[0]
        for tap_index, (row_shift, col_shift) in enumerate(TAPS):
            window = grad_padded[
                :, 1 - row_shift : 1 - row_shift + row_count, 1 - col_shift : 1 - col_shift + col_count
            ].reshape(count_rows, pixels)
            running = running + lax.dot_general(
                shard_piece[:, tap_index, :],
                window,
                (((0,), (0,)), ((), ())),
                preferred_element_type=jnp.float32,
            )
        return (
            latent.reshape(lat_local, row_count, col_count),
            running.reshape(in_local, row_count, col_count),
            grad_gamma,
            grad_beta,
        )

    return per_device


def solution(mesh):
    return jax.shard_map(
        make_per_device(ring_order(mesh)),
        mesh=mesh,
        in_specs=(
            P("chan", ("grp", "row"), None),
            P("row", None, "chan"),
            P("chan", None),
            P("chan"),
            P("chan", ("grp", "row"), None),
        ),
        out_specs=(
            P("chan", ("grp", "row"), None),
            P("chan", ("grp", "row"), None),
            P(("grp", "chan"), None),
            P(("grp", "chan")),
        ),
        check_vma=False,
    )
```

```python
import math

import jax
import jax.numpy as jnp
from jax import lax
from jax.sharding import PartitionSpec as P

TAPS = ((-1, -1), (-1, 0), (-1, 1), (0, -1), (0, 0), (0, 1), (1, -1), (1, 0), (1, 1))
SWAP = [(0, 1), (1, 0)]


def extended(shard, sides, width):
    for axis, dim in sides:
        count, length = (lax.axis_size(axis), shard.shape[dim])
        up = [(i, (i + 1) % count) for i in range(count - 1)]
        down = [(j, i) for i, j in up]
        last = lax.slice_in_dim(shard, length - width, length, axis=dim)
        leading = lax.slice_in_dim(shard, 0, width, axis=dim)
        before = lax.ppermute(last, axis, up)
        after = lax.ppermute(leading, axis, down)
        shard = jnp.concatenate([before, shard, after], axis=dim)
    return shard


def chan_gather(x):
    other = lax.ppermute(x, "chan", SWAP)
    both = jnp.concatenate([x, other], 0)
    return jnp.roll(both, lax.axis_index("chan") * x.shape[0], axis=0)


def chan_gather_into(mine, other):
    both = jnp.concatenate([mine, other], 0)
    return jnp.roll(both, lax.axis_index("chan") * mine.shape[0], axis=0)


def chan_scatter_sum(x):
    half = x.shape[0] // 2
    index = lax.axis_index("chan")
    mine = lax.dynamic_slice_in_dim(x, index * half, half, 0)
    theirs = lax.dynamic_slice_in_dim(x, (1 - index) * half, half, 0)
    return mine + lax.ppermute(theirs, "chan", SWAP)


def ring_order(mesh):
    count = mesh.shape["row"]
    try:
        coords = [tuple(d.coords) for d in mesh.devices[0, :, 0]]
    except Exception:
        return list(range(count))
    xs = sorted({c[0] for c in coords})
    zs = sorted({c[2] for c in coords})
    if len(xs) * len(zs) != count or len(zs) % 2:
        return list(range(count))
    where = {(c[0], c[2]): i for i, c in enumerate(coords)}
    path = [where[(xs[0], zs[0])]]
    for k, z in enumerate(zs):
        cols = xs[1:] if k % 2 == 0 else xs[:0:-1]
        path += [where[(x, z)] for x in cols]
    path += [where[(xs[0], z)] for z in zs[:0:-1]]
    return path if len(set(path)) == count else list(range(count))


def ring_sum(x, ring):
    count = len(ring)
    forward = [(ring[i], ring[(i + 1) % count]) for i in range(count)]
    backward = [(b, a) for a, b in forward]
    ring_index = jnp.asarray(ring, jnp.int32)
    position = jnp.asarray([ring.index(i) for i in range(count)], jnp.int32)[lax.axis_index("row")]
    rows = x.shape[0] // (2 * count)
    blocks = x.reshape((count, 2, rows) + x.shape[1:])
    moves = (forward, backward)
    signs = (1, -1)

    def pick(part, step):
        index = ring_index[(position - signs[part] * (1 + step)) % count]
        return lax.dynamic_index_in_dim(blocks, index, 0, keepdims=False)[part]

    carry = [pick(part, 0) for part in range(2)]
    for step in range(1, count):
        for part in range(2):
            carry[part] = lax.ppermute(carry[part], "row", moves[part]) + pick(part, step)
    own = jnp.concatenate(carry, 0).astype(jnp.bfloat16)
    return lax.all_gather(own, "row", axis=0, tiled=True).astype(jnp.float32)


def make_per_device(ring):
    def per_device(band_strip, conv_weight, gdn_gamma, gdn_beta, cotangent):
        in_local = band_strip.shape[0]
        row_count = band_strip.shape[1]
        col_count = band_strip.shape[2]
        pixels = row_count * col_count
        lat_local = gdn_gamma.shape[0]
        rimmed = extended(band_strip, (("row", 1),), 1)
        strip_padded = jnp.pad(rimmed, ((0, 0), (0, 0), (1, 1)))
        shard_piece = lax.all_gather(conv_weight, "row", axis=0, tiled=True)
        partial_value = jnp.zeros((shard_piece.shape[0], pixels), jnp.float32)
        for tap_index, (row_shift, col_shift) in enumerate(TAPS):
            window = strip_padded[
                :, 1 + row_shift : 1 + row_shift + row_count, 1 + col_shift : 1 + col_shift + col_count
            ].reshape(in_local, pixels)
            partial_value = partial_value + jnp.dot(
                shard_piece[:, tap_index, :], window, preferred_element_type=jnp.float32
            )
        pre = lax.psum_scatter(partial_value, "chan", scatter_dimension=0, tiled=True)
        squares_own = (pre * pre).astype(jnp.bfloat16)
        squares = chan_gather(squares_own)
        norm_value = gdn_beta[:, None] + jnp.dot(gdn_gamma, squares, preferred_element_type=jnp.float32)
        inverse = lax.rsqrt(norm_value)
        latent = (pre * inverse).astype(jnp.bfloat16)
        upstream = cotangent.reshape(lat_local, pixels).astype(jnp.float32)
        shares = (-0.5 * upstream * pre * inverse * inverse * inverse).astype(jnp.bfloat16)
        index = lax.axis_index("chan")
        gamma_mine = lax.dynamic_slice_in_dim(gdn_gamma, index * lat_local, lat_local, 1)
        gamma_theirs = lax.dynamic_slice_in_dim(gdn_gamma, (1 - index) * lat_local, lat_local, 1)
        gamma_cols = chan_gather_into(gamma_mine, lax.ppermute(gamma_theirs, "chan", SWAP))
        shares_all = chan_gather(shares)
        back_sum = lax.dot_general(
            gamma_cols, shares_all, (((0,), (0,)), ((), ())), preferred_element_type=jnp.float32
        )
        latent_grad = (upstream * inverse + 2.0 * pre * back_sum).astype(jnp.bfloat16)
        lat_all = squares.shape[0]
        squares_ones = jnp.concatenate([squares, jnp.ones((128, pixels), squares.dtype)], 0)
        joined = lax.dot_general(
            shares, squares_ones, (((1,), (1,)), ((), ())), preferred_element_type=jnp.float32
        )
        if len(ring) <= 16:
            joined_total = ring_sum(joined, ring)
        else:
            joined_total = lax.psum(joined, "row")
        gamma_total = joined_total[:, :lat_all]
        beta_total = joined_total[:, lat_all]
        scale_factor = 1.0 / math.sqrt(pixels * lax.axis_size("row"))
        grad_gamma = gamma_total * scale_factor
        grad_beta = beta_total * scale_factor
        grad_all = chan_gather(latent_grad.reshape(lat_local, row_count, col_count))
        grad_rimmed = extended(grad_all, (("row", 1),), 1)
        grad_padded = jnp.pad(grad_rimmed, ((0, 0), (0, 0), (1, 1)))
        running = jnp.zeros((in_local, pixels), jnp.float32)
        count_rows = shard_piece.shape[0]
        for tap_index, (row_shift, col_shift) in enumerate(TAPS):
            window = grad_padded[
                :, 1 - row_shift : 1 - row_shift + row_count, 1 - col_shift : 1 - col_shift + col_count
            ].reshape(count_rows, pixels)
            running = running + lax.dot_general(
                shard_piece[:, tap_index, :],
                window,
                (((0,), (0,)), ((), ())),
                preferred_element_type=jnp.float32,
            )
        return (
            latent.reshape(lat_local, row_count, col_count),
            running.reshape(in_local, row_count, col_count),
            grad_gamma,
            grad_beta,
        )

    return per_device


def solution(mesh):
    return jax.shard_map(
        make_per_device(ring_order(mesh)),
        mesh=mesh,
        in_specs=(
            P("chan", ("grp", "row"), None),
            P("row", None, "chan"),
            P("chan", None),
            P("chan"),
            P("chan", ("grp", "row"), None),
        ),
        out_specs=(
            P("chan", ("grp", "row"), None),
            P("chan", ("grp", "row"), None),
            P(("grp", "chan"), None),
            P(("grp", "chan")),
        ),
        check_vma=False,
    )
```

```python
import math

import jax
import jax.numpy as jnp
from jax import lax
from jax.sharding import PartitionSpec as P

TAPS = ((-1, -1), (-1, 0), (-1, 1), (0, -1), (0, 0), (0, 1), (1, -1), (1, 0), (1, 1))
SWAP = [(0, 1), (1, 0)]


def extended(shard, sides, width):
    for axis, dim in sides:
        count, length = (lax.axis_size(axis), shard.shape[dim])
        up = [(i, (i + 1) % count) for i in range(count - 1)]
        down = [(j, i) for i, j in up]
        last = lax.slice_in_dim(shard, length - width, length, axis=dim)
        leading = lax.slice_in_dim(shard, 0, width, axis=dim)
        before = lax.ppermute(last, axis, up)
        after = lax.ppermute(leading, axis, down)
        shard = jnp.concatenate([before, shard, after], axis=dim)
    return shard


def chan_gather(x):
    other = lax.ppermute(x, "chan", SWAP)
    both = jnp.concatenate([x, other], 0)
    return jnp.roll(both, lax.axis_index("chan") * x.shape[0], axis=0)


def chan_gather_into(mine, other):
    both = jnp.concatenate([mine, other], 0)
    return jnp.roll(both, lax.axis_index("chan") * mine.shape[0], axis=0)


def chan_scatter_sum(x):
    half = x.shape[0] // 2
    index = lax.axis_index("chan")
    mine = lax.dynamic_slice_in_dim(x, index * half, half, 0)
    theirs = lax.dynamic_slice_in_dim(x, (1 - index) * half, half, 0)
    return mine + lax.ppermute(theirs, "chan", SWAP)


def ring_order(mesh):
    count = mesh.shape["row"]
    try:
        coords = [tuple(d.coords) for d in mesh.devices[0, :, 0]]
    except Exception:
        return list(range(count))
    xs = sorted({c[0] for c in coords})
    zs = sorted({c[2] for c in coords})
    if len(xs) * len(zs) != count or len(zs) % 2:
        return list(range(count))
    where = {(c[0], c[2]): i for i, c in enumerate(coords)}
    path = [where[(xs[0], zs[0])]]
    for k, z in enumerate(zs):
        cols = xs[1:] if k % 2 == 0 else xs[:0:-1]
        path += [where[(x, z)] for x in cols]
    path += [where[(xs[0], z)] for z in zs[:0:-1]]
    return path if len(set(path)) == count else list(range(count))


def ring_sum(blocks, ring, hold):
    count = len(ring)
    forward = [(ring[i], ring[(i + 1) % count]) for i in range(count)]
    backward = [(b, a) for a, b in forward]
    position = jnp.asarray([ring.index(i) for i in range(count)], jnp.int32)[lax.axis_index("row")]

    def chunks(x, part):
        half = x.shape[0] // 2
        piece = x[part * half : (part + 1) * half]
        return piece.reshape((count, half // count) + x.shape[1:])

    split = [[chunks(x, part) for x in blocks] for part in range(2)]
    moves = (forward, backward)
    signs = (1, -1)

    def pick(part, step):
        index = (position - signs[part] * (1 + step)) % count
        return [jnp.take(c, index, axis=0) for c in split[part]]

    carry = [pick(part, 0) for part in range(2)]
    for step in range(1, count):
        for part in range(2):
            got = lax.ppermute(carry[part], "row", moves[part])
            carry[part] = [g + o for g, o in zip(got, pick(part, step))]
        if step == 1:
            hold, carry = lax.optimization_barrier((hold, carry))
    gathered = [[c.astype(jnp.bfloat16) for c in part] for part in carry]
    gathered = [[c] for c in gathered]
    for step in range(1, count):
        for part in range(2):
            gathered[part].append(lax.ppermute(gathered[part][-1], "row", moves[part]))
    results = []
    for leaf in range(len(blocks)):
        halves = []
        for part in range(2):
            stacked = jnp.stack([g[leaf] for g in gathered[part]], 0)
            order = (signs[part] * (position - jnp.arange(count))) % count
            halves.append(jnp.take(stacked, order, axis=0).reshape((-1,) + stacked.shape[2:]))
        results.append(jnp.concatenate(halves, 0).astype(jnp.float32))
    return results, hold


def make_per_device(ring):
    def per_device(band_strip, conv_weight, gdn_gamma, gdn_beta, cotangent):
        in_local = band_strip.shape[0]
        row_count = band_strip.shape[1]
        col_count = band_strip.shape[2]
        pixels = row_count * col_count
        lat_local = gdn_gamma.shape[0]
        rimmed = extended(band_strip, (("row", 1),), 1)
        strip_padded = jnp.pad(rimmed, ((0, 0), (0, 0), (1, 1)))
        shard_piece = lax.all_gather(conv_weight, "row", axis=0, tiled=True)
        partial_value = jnp.zeros((shard_piece.shape[0], pixels), jnp.float32)
        for tap_index, (row_shift, col_shift) in enumerate(TAPS):
            window = strip_padded[
                :, 1 + row_shift : 1 + row_shift + row_count, 1 + col_shift : 1 + col_shift + col_count
            ].reshape(in_local, pixels)
            partial_value = partial_value + jnp.dot(
                shard_piece[:, tap_index, :], window, preferred_element_type=jnp.float32
            )
        pre = lax.psum_scatter(partial_value, "chan", scatter_dimension=0, tiled=True)
        squares_own = (pre * pre).astype(jnp.bfloat16)
        squares = chan_gather(squares_own)
        norm_value = gdn_beta[:, None] + jnp.dot(gdn_gamma, squares, preferred_element_type=jnp.float32)
        inverse = lax.rsqrt(norm_value)
        scaled = pre * inverse
        upstream = cotangent.reshape(lat_local, pixels).astype(jnp.float32)
        shares = (-0.5 * upstream * pre * inverse * inverse * inverse).astype(jnp.bfloat16)
        index = lax.axis_index("chan")
        gamma_mine = lax.dynamic_slice_in_dim(gdn_gamma, index * lat_local, lat_local, 1)
        gamma_theirs = lax.dynamic_slice_in_dim(gdn_gamma, (1 - index) * lat_local, lat_local, 1)
        gamma_cols = chan_gather_into(gamma_mine, lax.ppermute(gamma_theirs, "chan", SWAP))
        shares_all = chan_gather(shares)
        back_sum = lax.dot_general(
            gamma_cols, shares_all, (((0,), (0,)), ((), ())), preferred_element_type=jnp.float32
        )
        latent_grad = (upstream * inverse + 2.0 * pre * back_sum).astype(jnp.bfloat16)
        lat_all = squares.shape[0]
        squares_ones = jnp.concatenate([squares, jnp.ones((128, pixels), squares.dtype)], 0)
        joined = lax.dot_general(
            shares, squares_ones, (((1,), (1,)), ((), ())), preferred_element_type=jnp.float32
        )
        if len(ring) <= 16:
            (joined_total,), scaled = ring_sum([joined], ring, scaled)
        else:
            joined_total = lax.psum(joined, "row")
        latent = scaled.astype(jnp.bfloat16)
        gamma_total = joined_total[:, :lat_all]
        beta_total = joined_total[:, lat_all]
        scale_factor = 1.0 / math.sqrt(pixels * lax.axis_size("row"))
        grad_gamma = gamma_total * scale_factor
        grad_beta = beta_total * scale_factor
        grad_all = chan_gather(latent_grad.reshape(lat_local, row_count, col_count))
        grad_rimmed = extended(grad_all, (("row", 1),), 1)
        grad_padded = jnp.pad(grad_rimmed, ((0, 0), (0, 0), (1, 1)))
        running = jnp.zeros((in_local, pixels), jnp.float32)
        count_rows = shard_piece.shape[0]
        for tap_index, (row_shift, col_shift) in enumerate(TAPS):
            window = grad_padded[
                :, 1 - row_shift : 1 - row_shift + row_count, 1 - col_shift : 1 - col_shift + col_count
            ].reshape(count_rows, pixels)
            running = running + lax.dot_general(
                shard_piece[:, tap_index, :],
                window,
                (((0,), (0,)), ((), ())),
                preferred_element_type=jnp.float32,
            )
        return (
            latent.reshape(lat_local, row_count, col_count),
            running.reshape(in_local, row_count, col_count),
            grad_gamma,
            grad_beta,
        )

    return per_device


def solution(mesh):
    return jax.shard_map(
        make_per_device(ring_order(mesh)),
        mesh=mesh,
        in_specs=(
            P("chan", ("grp", "row"), None),
            P("row", None, "chan"),
            P("chan", None),
            P("chan"),
            P("chan", ("grp", "row"), None),
        ),
        out_specs=(
            P("chan", ("grp", "row"), None),
            P("chan", ("grp", "row"), None),
            P(("grp", "chan"), None),
            P(("grp", "chan")),
        ),
        check_vma=False,
    )
```

```python
import math

import jax
import jax.numpy as jnp
from jax import lax
from jax.sharding import PartitionSpec as P

TAPS = ((-1, -1), (-1, 0), (-1, 1), (0, -1), (0, 0), (0, 1), (1, -1), (1, 0), (1, 1))
SWAP = [(0, 1), (1, 0)]


def extended(shard, sides, width):
    for axis, dim in sides:
        count, length = (lax.axis_size(axis), shard.shape[dim])
        up = [(i, (i + 1) % count) for i in range(count - 1)]
        down = [(j, i) for i, j in up]
        last = lax.slice_in_dim(shard, length - width, length, axis=dim)
        leading = lax.slice_in_dim(shard, 0, width, axis=dim)
        before = lax.ppermute(last, axis, up)
        after = lax.ppermute(leading, axis, down)
        shard = jnp.concatenate([before, shard, after], axis=dim)
    return shard


def chan_gather(x):
    other = lax.ppermute(x, "chan", SWAP)
    both = jnp.concatenate([x, other], 0)
    return jnp.roll(both, lax.axis_index("chan") * x.shape[0], axis=0)


def chan_scatter_sum(x):
    half = x.shape[0] // 2
    index = lax.axis_index("chan")
    mine = lax.dynamic_slice_in_dim(x, index * half, half, 0)
    theirs = lax.dynamic_slice_in_dim(x, (1 - index) * half, half, 0)
    return mine + lax.ppermute(theirs, "chan", SWAP)


def ring_order(mesh):
    count = mesh.shape["row"]
    try:
        coords = [tuple(d.coords) for d in mesh.devices[0, :, 0]]
    except Exception:
        return list(range(count))
    xs = sorted({c[0] for c in coords})
    zs = sorted({c[2] for c in coords})
    if len(xs) * len(zs) != count or len(zs) % 2:
        return list(range(count))
    where = {(c[0], c[2]): i for i, c in enumerate(coords)}
    path = [where[(xs[0], zs[0])]]
    for k, z in enumerate(zs):
        cols = xs[1:] if k % 2 == 0 else xs[:0:-1]
        path += [where[(x, z)] for x in cols]
    path += [where[(xs[0], z)] for z in zs[:0:-1]]
    return path if len(set(path)) == count else list(range(count))


def ring_sum(blocks, ring):
    count = len(ring)
    forward = [(ring[i], ring[(i + 1) % count]) for i in range(count)]
    backward = [(b, a) for a, b in forward]
    position = jnp.asarray([ring.index(i) for i in range(count)], jnp.int32)[lax.axis_index("row")]

    def chunks(x, part):
        half = x.shape[0] // 2
        piece = x[part * half : (part + 1) * half]
        return piece.reshape((count, half // count) + x.shape[1:])

    split = [[chunks(x, part) for x in blocks] for part in range(2)]
    moves = (forward, backward)
    signs = (1, -1)

    def pick(part, step):
        index = (position - signs[part] * (1 + step)) % count
        return [jnp.take(c, index, axis=0) for c in split[part]]

    carry = [pick(part, 0) for part in range(2)]
    for step in range(1, count):
        for part in range(2):
            got = lax.ppermute(carry[part], "row", moves[part])
            carry[part] = [g + o for g, o in zip(got, pick(part, step))]
    gathered = [[c.astype(jnp.bfloat16) for c in part] for part in carry]
    gathered = [[c] for c in gathered]
    for step in range(1, count):
        for part in range(2):
            gathered[part].append(lax.ppermute(gathered[part][-1], "row", moves[part]))
    results = []
    for leaf in range(len(blocks)):
        halves = []
        for part in range(2):
            stacked = jnp.stack([g[leaf] for g in gathered[part]], 0)
            order = (signs[part] * (position - jnp.arange(count))) % count
            halves.append(jnp.take(stacked, order, axis=0).reshape((-1,) + stacked.shape[2:]))
        results.append(jnp.concatenate(halves, 0).astype(jnp.float32))
    return results


def make_per_device(ring):
    def per_device(band_strip, conv_weight, gdn_gamma, gdn_beta, cotangent):
        in_local = band_strip.shape[0]
        row_count = band_strip.shape[1]
        col_count = band_strip.shape[2]
        pixels = row_count * col_count
        lat_local = gdn_gamma.shape[0]
        rimmed = extended(band_strip, (("row", 1),), 1)
        strip_padded = jnp.pad(rimmed, ((0, 0), (0, 0), (1, 1)))
        shard_piece = lax.all_gather(conv_weight, "row", axis=0, tiled=True)
        partial_value = jnp.zeros((shard_piece.shape[0], pixels), jnp.float32)
        for tap_index, (row_shift, col_shift) in enumerate(TAPS):
            window = strip_padded[
                :, 1 + row_shift : 1 + row_shift + row_count, 1 + col_shift : 1 + col_shift + col_count
            ].reshape(in_local, pixels)
            partial_value = partial_value + jnp.dot(
                shard_piece[:, tap_index, :], window, preferred_element_type=jnp.float32
            )
        pre = lax.psum_scatter(partial_value, "chan", scatter_dimension=0, tiled=True)
        index = lax.axis_index("chan")
        gamma_mine = lax.dynamic_slice_in_dim(gdn_gamma, index * lat_local, lat_local, 1)
        gamma_theirs = lax.dynamic_slice_in_dim(gdn_gamma, (1 - index) * lat_local, lat_local, 1)
        gamma_local = jnp.concatenate([gamma_mine, gamma_theirs], 1)
        squares_own = (pre * pre).astype(jnp.bfloat16)
        squares = jnp.concatenate([squares_own, lax.ppermute(squares_own, "chan", SWAP)], 0)
        norm_value = gdn_beta[:, None] + jnp.dot(gamma_local, squares, preferred_element_type=jnp.float32)
        inverse = lax.rsqrt(norm_value)
        latent = (pre * inverse).astype(jnp.bfloat16)
        upstream = cotangent.reshape(lat_local, pixels).astype(jnp.float32)
        shares = (-0.5 * upstream * pre * inverse * inverse * inverse).astype(jnp.bfloat16)
        gamma_cols = jnp.concatenate([gamma_mine, lax.ppermute(gamma_theirs, "chan", SWAP)], 0)
        shares_all = jnp.concatenate([shares, lax.ppermute(shares, "chan", SWAP)], 0)
        back_sum = lax.dot_general(
            gamma_cols, shares_all, (((0,), (0,)), ((), ())), preferred_element_type=jnp.float32
        )
        latent_grad = (upstream * inverse + 2.0 * pre * back_sum).astype(jnp.bfloat16)
        lat_all = squares.shape[0]
        squares_ones = jnp.concatenate([squares, jnp.ones((128, pixels), squares.dtype)], 0)
        joined = lax.dot_general(
            shares, squares_ones, (((1,), (1,)), ((), ())), preferred_element_type=jnp.float32
        )
        if len(ring) <= 16:
            (joined_total,) = ring_sum([joined], ring)
        else:
            joined_total = lax.psum(joined, "row")
        gamma_total = jnp.roll(joined_total[:, :lat_all], index * lat_local, axis=1)
        beta_total = joined_total[:, lat_all]
        scale_factor = 1.0 / math.sqrt(pixels * lax.axis_size("row"))
        grad_gamma = gamma_total * scale_factor
        grad_beta = beta_total * scale_factor
        grad_all = chan_gather(latent_grad.reshape(lat_local, row_count, col_count))
        grad_rimmed = extended(grad_all, (("row", 1),), 1)
        grad_padded = jnp.pad(grad_rimmed, ((0, 0), (0, 0), (1, 1)))
        running = jnp.zeros((in_local, pixels), jnp.float32)
        count_rows = shard_piece.shape[0]
        for tap_index, (row_shift, col_shift) in enumerate(TAPS):
            window = grad_padded[
                :, 1 - row_shift : 1 - row_shift + row_count, 1 - col_shift : 1 - col_shift + col_count
            ].reshape(count_rows, pixels)
            running = running + lax.dot_general(
                shard_piece[:, tap_index, :],
                window,
                (((0,), (0,)), ((), ())),
                preferred_element_type=jnp.float32,
            )
        return (
            latent.reshape(lat_local, row_count, col_count),
            running.reshape(in_local, row_count, col_count),
            grad_gamma,
            grad_beta,
        )

    return per_device


def solution(mesh):
    return jax.shard_map(
        make_per_device(ring_order(mesh)),
        mesh=mesh,
        in_specs=(
            P("chan", ("grp", "row"), None),
            P("row", None, "chan"),
            P("chan", None),
            P("chan"),
            P("chan", ("grp", "row"), None),
        ),
        out_specs=(
            P("chan", ("grp", "row"), None),
            P("chan", ("grp", "row"), None),
            P(("grp", "chan"), None),
            P(("grp", "chan")),
        ),
        check_vma=False,
    )
```

```python
import math

import jax
import jax.numpy as jnp
from jax import lax
from jax.sharding import PartitionSpec as P

TAPS = ((-1, -1), (-1, 0), (-1, 1), (0, -1), (0, 0), (0, 1), (1, -1), (1, 0), (1, 1))
SWAP = [(0, 1), (1, 0)]


def extended(shard, sides, width):
    for axis, dim in sides:
        count, length = (lax.axis_size(axis), shard.shape[dim])
        up = [(i, (i + 1) % count) for i in range(count - 1)]
        down = [(j, i) for i, j in up]
        last = lax.slice_in_dim(shard, length - width, length, axis=dim)
        leading = lax.slice_in_dim(shard, 0, width, axis=dim)
        before = lax.ppermute(last, axis, up)
        after = lax.ppermute(leading, axis, down)
        shard = jnp.concatenate([before, shard, after], axis=dim)
    return shard


def chan_gather(x):
    other = lax.ppermute(x, "chan", SWAP)
    both = jnp.concatenate([x, other], 0)
    return jnp.roll(both, lax.axis_index("chan") * x.shape[0], axis=0)


def chan_gather_into(mine, other):
    both = jnp.concatenate([mine, other], 0)
    return jnp.roll(both, lax.axis_index("chan") * mine.shape[0], axis=0)


def chan_scatter_sum(x):
    half = x.shape[0] // 2
    index = lax.axis_index("chan")
    mine = lax.dynamic_slice_in_dim(x, index * half, half, 0)
    theirs = lax.dynamic_slice_in_dim(x, (1 - index) * half, half, 0)
    return mine + lax.ppermute(theirs, "chan", SWAP)


def ring_order(mesh):
    count = mesh.shape["row"]
    try:
        coords = [tuple(d.coords) for d in mesh.devices[0, :, 0]]
    except Exception:
        return list(range(count))
    xs = sorted({c[0] for c in coords})
    zs = sorted({c[2] for c in coords})
    if len(xs) * len(zs) != count or len(zs) % 2:
        return list(range(count))
    where = {(c[0], c[2]): i for i, c in enumerate(coords)}
    path = [where[(xs[0], zs[0])]]
    for k, z in enumerate(zs):
        cols = xs[1:] if k % 2 == 0 else xs[:0:-1]
        path += [where[(x, z)] for x in cols]
    path += [where[(xs[0], z)] for z in zs[:0:-1]]
    return path if len(set(path)) == count else list(range(count))


def ring_sum(blocks, ring):
    count = len(ring)
    forward = [(ring[i], ring[(i + 1) % count]) for i in range(count)]
    backward = [(b, a) for a, b in forward]
    position = jnp.asarray([ring.index(i) for i in range(count)], jnp.int32)[lax.axis_index("row")]

    def chunks(x, part):
        half = x.shape[0] // 2
        piece = x[part * half : (part + 1) * half]
        return piece.reshape((count, half // count) + x.shape[1:])

    split = [[chunks(x, part) for x in blocks] for part in range(2)]
    moves = (forward, backward)
    signs = (1, -1)

    def pick(part, step):
        index = (position - signs[part] * (1 + step)) % count
        return [jnp.take(c, index, axis=0) for c in split[part]]

    carry = [pick(part, 0) for part in range(2)]
    for step in range(1, count):
        for part in range(2):
            got = lax.ppermute(carry[part], "row", moves[part])
            carry[part] = [g + o for g, o in zip(got, pick(part, step))]
    gathered = [[c.astype(jnp.bfloat16) for c in part] for part in carry]
    gathered = [[c] for c in gathered]
    for step in range(1, count):
        for part in range(2):
            gathered[part].append(lax.ppermute(gathered[part][-1], "row", moves[part]))
    results = []
    for leaf in range(len(blocks)):
        halves = []
        for part in range(2):
            stacked = jnp.stack([g[leaf] for g in gathered[part]], 0)
            order = (signs[part] * (position - jnp.arange(count))) % count
            halves.append(jnp.take(stacked, order, axis=0).reshape((-1,) + stacked.shape[2:]))
        results.append(jnp.concatenate(halves, 0).astype(jnp.float32))
    return results


def make_per_device(ring):
    def per_device(band_strip, conv_weight, gdn_gamma, gdn_beta, cotangent):
        in_local = band_strip.shape[0]
        row_count = band_strip.shape[1]
        col_count = band_strip.shape[2]
        pixels = row_count * col_count
        lat_local = gdn_gamma.shape[0]
        rimmed = extended(band_strip, (("row", 1),), 1)
        strip_padded = jnp.pad(rimmed, ((0, 0), (0, 0), (1, 1)))
        shard_piece = lax.all_gather(conv_weight, "row", axis=0, tiled=True)
        partial_value = jnp.zeros((shard_piece.shape[0], pixels), jnp.float32)
        for tap_index, (row_shift, col_shift) in enumerate(TAPS):
            window = strip_padded[
                :, 1 + row_shift : 1 + row_shift + row_count, 1 + col_shift : 1 + col_shift + col_count
            ].reshape(in_local, pixels)
            partial_value = partial_value + jnp.dot(
                shard_piece[:, tap_index, :], window, preferred_element_type=jnp.float32
            )
        pre = lax.psum_scatter(partial_value, "chan", scatter_dimension=0, tiled=True)
        squares_own = (pre * pre).astype(jnp.bfloat16)
        squares = chan_gather(squares_own)
        norm_value = gdn_beta[:, None] + jnp.dot(gdn_gamma, squares, preferred_element_type=jnp.float32)
        inverse = lax.rsqrt(norm_value)
        latent = (pre * inverse).astype(jnp.bfloat16)
        upstream = cotangent.reshape(lat_local, pixels).astype(jnp.float32)
        shares = (-0.5 * upstream * pre * inverse * inverse * inverse).astype(jnp.bfloat16)
        index = lax.axis_index("chan")
        gamma_mine = lax.dynamic_slice_in_dim(gdn_gamma, index * lat_local, lat_local, 1)
        gamma_theirs = lax.dynamic_slice_in_dim(gdn_gamma, (1 - index) * lat_local, lat_local, 1)
        gamma_cols = chan_gather_into(gamma_mine, lax.ppermute(gamma_theirs, "chan", SWAP))
        shares_all = chan_gather(shares)
        back_sum = lax.dot_general(
            gamma_cols, shares_all, (((0,), (0,)), ((), ())), preferred_element_type=jnp.float32
        )
        latent_grad = (upstream * inverse + 2.0 * pre * back_sum).astype(jnp.bfloat16)
        lat_all = squares.shape[0]
        squares_ones = jnp.concatenate([squares, jnp.ones((128, pixels), squares.dtype)], 0)
        joined = lax.dot_general(
            shares, squares_ones, (((1,), (1,)), ((), ())), preferred_element_type=jnp.float32
        )
        if len(ring) <= 16:
            (joined_total,) = ring_sum([joined], ring)
        else:
            joined_total = lax.psum(joined, "row")
        gamma_total = joined_total[:, :lat_all]
        beta_total = joined_total[:, lat_all]
        scale_factor = 1.0 / math.sqrt(pixels * lax.axis_size("row"))
        grad_gamma = gamma_total * scale_factor
        grad_beta = beta_total * scale_factor
        grad_all = chan_gather(latent_grad.reshape(lat_local, row_count, col_count))
        grad_padded = jnp.pad(grad_all, ((0, 0), (1, 1), (1, 1)))
        running = jnp.zeros((in_local, pixels), jnp.float32)
        count_rows = shard_piece.shape[0]
        to_next = jnp.zeros((in_local, col_count), jnp.float32)
        to_prev = jnp.zeros((in_local, col_count), jnp.float32)
        for tap_index, (row_shift, col_shift) in enumerate(TAPS):
            window = grad_padded[
                :, 1 - row_shift : 1 - row_shift + row_count, 1 - col_shift : 1 - col_shift + col_count
            ].reshape(count_rows, pixels)
            weights = shard_piece[:, tap_index, :]
            contract = (((0,), (0,)), ((), ()))
            running = running + lax.dot_general(
                weights, window, contract, preferred_element_type=jnp.float32
            )
            if row_shift != 0:
                edge = row_count if row_shift == 1 else 1
                line = grad_padded[:, edge, 1 - col_shift : 1 - col_shift + col_count]
                part = lax.dot_general(weights, line, contract, preferred_element_type=jnp.float32)
                if row_shift == 1:
                    to_next = to_next + part
                else:
                    to_prev = to_prev + part
        count = lax.axis_size("row")
        up = [(i, i + 1) for i in range(count - 1)]
        down = [(j, i) for i, j in up]
        from_prev = lax.ppermute(to_next, "row", up)
        from_next = lax.ppermute(to_prev, "row", down)
        running = running.reshape(in_local, row_count, col_count)
        running = running.at[:, 0].add(from_prev).at[:, row_count - 1].add(from_next)
        running = running.reshape(in_local, pixels)
        return (
            latent.reshape(lat_local, row_count, col_count),
            running.reshape(in_local, row_count, col_count),
            grad_gamma,
            grad_beta,
        )

    return per_device


def solution(mesh):
    return jax.shard_map(
        make_per_device(ring_order(mesh)),
        mesh=mesh,
        in_specs=(
            P("chan", ("grp", "row"), None),
            P("row", None, "chan"),
            P("chan", None),
            P("chan"),
            P("chan", ("grp", "row"), None),
        ),
        out_specs=(
            P("chan", ("grp", "row"), None),
            P("chan", ("grp", "row"), None),
            P(("grp", "chan"), None),
            P(("grp", "chan")),
        ),
        check_vma=False,
    )
```

```python
import math

import jax
import jax.numpy as jnp
from jax import lax
from jax.sharding import PartitionSpec as P

TAPS = ((-1, -1), (-1, 0), (-1, 1), (0, -1), (0, 0), (0, 1), (1, -1), (1, 0), (1, 1))
SWAP = [(0, 1), (1, 0)]


def extended(shard, sides, width):
    for axis, dim in sides:
        count, length = (lax.axis_size(axis), shard.shape[dim])
        up = [(i, (i + 1) % count) for i in range(count - 1)]
        down = [(j, i) for i, j in up]
        last = lax.slice_in_dim(shard, length - width, length, axis=dim)
        leading = lax.slice_in_dim(shard, 0, width, axis=dim)
        before = lax.ppermute(last, axis, up)
        after = lax.ppermute(leading, axis, down)
        shard = jnp.concatenate([before, shard, after], axis=dim)
    return shard


def chan_gather(x):
    other = lax.ppermute(x, "chan", SWAP)
    both = jnp.concatenate([x, other], 0)
    return jnp.roll(both, lax.axis_index("chan") * x.shape[0], axis=0)


def chan_gather_into(mine, other):
    both = jnp.concatenate([mine, other], 0)
    return jnp.roll(both, lax.axis_index("chan") * mine.shape[0], axis=0)


def chan_scatter_sum(x):
    half = x.shape[0] // 2
    index = lax.axis_index("chan")
    mine = lax.dynamic_slice_in_dim(x, index * half, half, 0)
    theirs = lax.dynamic_slice_in_dim(x, (1 - index) * half, half, 0)
    return mine + lax.ppermute(theirs, "chan", SWAP)


def ring_order(mesh):
    count = mesh.shape["row"]
    try:
        coords = [tuple(d.coords) for d in mesh.devices[0, :, 0]]
    except Exception:
        return list(range(count))
    xs = sorted({c[0] for c in coords})
    zs = sorted({c[2] for c in coords})
    if len(xs) * len(zs) != count or len(zs) % 2:
        return list(range(count))
    where = {(c[0], c[2]): i for i, c in enumerate(coords)}
    path = [where[(xs[0], zs[0])]]
    for k, z in enumerate(zs):
        cols = xs[1:] if k % 2 == 0 else xs[:0:-1]
        path += [where[(x, z)] for x in cols]
    path += [where[(xs[0], z)] for z in zs[:0:-1]]
    return path if len(set(path)) == count else list(range(count))


def ring_sum(halves, ring):
    count = len(ring)
    forward = [(ring[i], ring[(i + 1) % count]) for i in range(count)]
    backward = [(b, a) for a, b in forward]
    position = jnp.asarray([ring.index(i) for i in range(count)], jnp.int32)[lax.axis_index("row")]
    split = [x.reshape((count, x.shape[0] // count) + x.shape[1:]) for x in halves]
    moves = (forward, backward)
    signs = (1, -1)

    def pick(part, step):
        index = (position - signs[part] * (1 + step)) % count
        return jnp.take(split[part], index, axis=0)

    carry = [pick(part, 0) for part in range(2)]
    for step in range(1, count):
        for part in range(2):
            carry[part] = lax.ppermute(carry[part], "row", moves[part]) + pick(part, step)
    gathered = [[c.astype(jnp.bfloat16)] for c in carry]
    for step in range(1, count):
        for part in range(2):
            gathered[part].append(lax.ppermute(gathered[part][-1], "row", moves[part]))
    results = []
    for part in range(2):
        stacked = jnp.stack(gathered[part], 0)
        order = (signs[part] * (position - jnp.arange(count))) % count
        results.append(jnp.take(stacked, order, axis=0).reshape((-1,) + stacked.shape[2:]))
    return [r.astype(jnp.float32) for r in results]


def make_per_device(ring):
    def per_device(band_strip, conv_weight, gdn_gamma, gdn_beta, cotangent):
        in_local = band_strip.shape[0]
        row_count = band_strip.shape[1]
        col_count = band_strip.shape[2]
        pixels = row_count * col_count
        lat_local = gdn_gamma.shape[0]
        rimmed = extended(band_strip, (("row", 1),), 1)
        strip_padded = jnp.pad(rimmed, ((0, 0), (0, 0), (1, 1)))
        shard_piece = lax.all_gather(conv_weight, "row", axis=0, tiled=True)
        partial_value = jnp.zeros((shard_piece.shape[0], pixels), jnp.float32)
        for tap_index, (row_shift, col_shift) in enumerate(TAPS):
            window = strip_padded[
                :, 1 + row_shift : 1 + row_shift + row_count, 1 + col_shift : 1 + col_shift + col_count
            ].reshape(in_local, pixels)
            partial_value = partial_value + jnp.dot(
                shard_piece[:, tap_index, :], window, preferred_element_type=jnp.float32
            )
        pre = lax.psum_scatter(partial_value, "chan", scatter_dimension=0, tiled=True)
        squares_own = (pre * pre).astype(jnp.bfloat16)
        squares = chan_gather(squares_own)
        norm_value = gdn_beta[:, None] + jnp.dot(gdn_gamma, squares, preferred_element_type=jnp.float32)
        inverse = lax.rsqrt(norm_value)
        latent = (pre * inverse).astype(jnp.bfloat16)
        upstream = cotangent.reshape(lat_local, pixels).astype(jnp.float32)
        shares = (-0.5 * upstream * pre * inverse * inverse * inverse).astype(jnp.bfloat16)
        index = lax.axis_index("chan")
        gamma_mine = lax.dynamic_slice_in_dim(gdn_gamma, index * lat_local, lat_local, 1)
        gamma_theirs = lax.dynamic_slice_in_dim(gdn_gamma, (1 - index) * lat_local, lat_local, 1)
        gamma_cols = chan_gather_into(gamma_mine, lax.ppermute(gamma_theirs, "chan", SWAP))
        shares_all = chan_gather(shares)
        back_sum = lax.dot_general(
            gamma_cols, shares_all, (((0,), (0,)), ((), ())), preferred_element_type=jnp.float32
        )
        latent_grad = (upstream * inverse + 2.0 * pre * back_sum).astype(jnp.bfloat16)
        lat_all = squares.shape[0]
        squares_ones = jnp.concatenate([squares, jnp.ones((128, pixels), squares.dtype)], 0)
        joined = lax.dot_general(
            shares, squares_ones, (((1,), (1,)), ((), ())), preferred_element_type=jnp.float32
        )
        if len(ring) <= 16:
            half = lat_local // 2
            first = joined[:half, :lat_all]
            second = joined[half:].at[:, lat_all + 1].set(joined[:half, lat_all])
            first_total, second_total = ring_sum([first, second], ring)
            gamma_total = jnp.concatenate([first_total, second_total[:, :lat_all]], 0)
            beta_total = jnp.concatenate([second_total[:, lat_all + 1], second_total[:, lat_all]], 0)
        else:
            joined_total = lax.psum(joined, "row")
            gamma_total = joined_total[:, :lat_all]
            beta_total = joined_total[:, lat_all]
        scale_factor = 1.0 / math.sqrt(pixels * lax.axis_size("row"))
        grad_gamma = gamma_total * scale_factor
        grad_beta = beta_total * scale_factor
        grad_all = chan_gather(latent_grad.reshape(lat_local, row_count, col_count))
        grad_rimmed = extended(grad_all, (("row", 1),), 1)
        grad_padded = jnp.pad(grad_rimmed, ((0, 0), (0, 0), (1, 1)))
        running = jnp.zeros((in_local, pixels), jnp.float32)
        count_rows = shard_piece.shape[0]
        for tap_index, (row_shift, col_shift) in enumerate(TAPS):
            window = grad_padded[
                :, 1 - row_shift : 1 - row_shift + row_count, 1 - col_shift : 1 - col_shift + col_count
            ].reshape(count_rows, pixels)
            running = running + lax.dot_general(
                shard_piece[:, tap_index, :],
                window,
                (((0,), (0,)), ((), ())),
                preferred_element_type=jnp.float32,
            )
        return (
            latent.reshape(lat_local, row_count, col_count),
            running.reshape(in_local, row_count, col_count),
            grad_gamma,
            grad_beta,
        )

    return per_device


def solution(mesh):
    return jax.shard_map(
        make_per_device(ring_order(mesh)),
        mesh=mesh,
        in_specs=(
            P("chan", ("grp", "row"), None),
            P("row", None, "chan"),
            P("chan", None),
            P("chan"),
            P("chan", ("grp", "row"), None),
        ),
        out_specs=(
            P("chan", ("grp", "row"), None),
            P("chan", ("grp", "row"), None),
            P(("grp", "chan"), None),
            P(("grp", "chan")),
        ),
        check_vma=False,
    )
```

```python
import math

import jax
import jax.numpy as jnp
from jax import lax
from jax.sharding import PartitionSpec as P

TAPS = ((-1, -1), (-1, 0), (-1, 1), (0, -1), (0, 0), (0, 1), (1, -1), (1, 0), (1, 1))
SWAP = [(0, 1), (1, 0)]


def extended(shard, sides, width):
    for axis, dim in sides:
        count, length = (lax.axis_size(axis), shard.shape[dim])
        up = [(i, (i + 1) % count) for i in range(count - 1)]
        down = [(j, i) for i, j in up]
        last = lax.slice_in_dim(shard, length - width, length, axis=dim)
        leading = lax.slice_in_dim(shard, 0, width, axis=dim)
        before = lax.ppermute(last, axis, up)
        after = lax.ppermute(leading, axis, down)
        shard = jnp.concatenate([before, shard, after], axis=dim)
    return shard


def chan_gather(x):
    other = lax.ppermute(x, "chan", SWAP)
    both = jnp.concatenate([x, other], 0)
    return jnp.roll(both, lax.axis_index("chan") * x.shape[0], axis=0)


def chan_gather_into(mine, other):
    both = jnp.concatenate([mine, other], 0)
    return jnp.roll(both, lax.axis_index("chan") * mine.shape[0], axis=0)


def chan_scatter_sum(x):
    half = x.shape[0] // 2
    index = lax.axis_index("chan")
    mine = lax.dynamic_slice_in_dim(x, index * half, half, 0)
    theirs = lax.dynamic_slice_in_dim(x, (1 - index) * half, half, 0)
    return mine + lax.ppermute(theirs, "chan", SWAP)


def ring_order(mesh):
    count = mesh.shape["row"]
    try:
        coords = [tuple(d.coords) for d in mesh.devices[0, :, 0]]
    except Exception:
        return list(range(count))
    xs = sorted({c[0] for c in coords})
    zs = sorted({c[2] for c in coords})
    if len(xs) * len(zs) != count or len(zs) % 2:
        return list(range(count))
    where = {(c[0], c[2]): i for i, c in enumerate(coords)}
    path = [where[(xs[0], zs[0])]]
    for k, z in enumerate(zs):
        cols = xs[1:] if k % 2 == 0 else xs[:0:-1]
        path += [where[(x, z)] for x in cols]
    path += [where[(xs[0], z)] for z in zs[:0:-1]]
    return path if len(set(path)) == count else list(range(count))


def ring_sum(blocks, ring):
    count = len(ring)
    forward = [(ring[i], ring[(i + 1) % count]) for i in range(count)]
    backward = [(b, a) for a, b in forward]
    position = jnp.asarray([ring.index(i) for i in range(count)], jnp.int32)[lax.axis_index("row")]

    def chunks(x, part):
        half = x.shape[0] // 2
        piece = x[part * half : (part + 1) * half]
        return piece.reshape((count, half // count) + x.shape[1:])

    split = [[chunks(x, part) for x in blocks] for part in range(2)]
    moves = (forward, backward)
    signs = (1, -1)

    def pick(part, step):
        index = (position - signs[part] * (1 + step)) % count
        return [jnp.take(c, index, axis=0) for c in split[part]]

    carry = [pick(part, 0) for part in range(2)]
    for step in range(1, count):
        for part in range(2):
            got = lax.ppermute(carry[part], "row", moves[part])
            carry[part] = [g + o for g, o in zip(got, pick(part, step))]
    gathered = [[c.astype(jnp.bfloat16) for c in part] for part in carry]
    gathered = [[c] for c in gathered]
    for step in range(1, count):
        for part in range(2):
            gathered[part].append(lax.ppermute(gathered[part][-1], "row", moves[part]))
    results = []
    for leaf in range(len(blocks)):
        halves = []
        for part in range(2):
            stacked = jnp.stack([g[leaf] for g in gathered[part]], 0)
            order = (signs[part] * (position - jnp.arange(count))) % count
            halves.append(jnp.take(stacked, order, axis=0).reshape((-1,) + stacked.shape[2:]))
        results.append(halves)
    return results


def make_per_device(ring):
    def per_device(band_strip, conv_weight, gdn_gamma, gdn_beta, cotangent):
        in_local = band_strip.shape[0]
        row_count = band_strip.shape[1]
        col_count = band_strip.shape[2]
        pixels = row_count * col_count
        lat_local = gdn_gamma.shape[0]
        rimmed = extended(band_strip, (("row", 1),), 1)
        strip_padded = jnp.pad(rimmed, ((0, 0), (0, 0), (1, 1)))
        shard_piece = lax.all_gather(conv_weight, "row", axis=0, tiled=True)
        partial_value = jnp.zeros((shard_piece.shape[0], pixels), jnp.float32)
        for tap_index, (row_shift, col_shift) in enumerate(TAPS):
            window = strip_padded[
                :, 1 + row_shift : 1 + row_shift + row_count, 1 + col_shift : 1 + col_shift + col_count
            ].reshape(in_local, pixels)
            partial_value = partial_value + jnp.dot(
                shard_piece[:, tap_index, :], window, preferred_element_type=jnp.float32
            )
        pre = lax.psum_scatter(partial_value, "chan", scatter_dimension=0, tiled=True)
        squares_own = (pre * pre).astype(jnp.bfloat16)
        squares = chan_gather(squares_own)
        norm_value = gdn_beta[:, None] + jnp.dot(gdn_gamma, squares, preferred_element_type=jnp.float32)
        inverse = lax.rsqrt(norm_value)
        latent = (pre * inverse).astype(jnp.bfloat16)
        upstream = cotangent.reshape(lat_local, pixels).astype(jnp.float32)
        shares = (-0.5 * upstream * pre * inverse * inverse * inverse).astype(jnp.bfloat16)
        index = lax.axis_index("chan")
        gamma_mine = lax.dynamic_slice_in_dim(gdn_gamma, index * lat_local, lat_local, 1)
        gamma_theirs = lax.dynamic_slice_in_dim(gdn_gamma, (1 - index) * lat_local, lat_local, 1)
        gamma_cols = chan_gather_into(gamma_mine, lax.ppermute(gamma_theirs, "chan", SWAP))
        shares_all = chan_gather(shares)
        back_sum = lax.dot_general(
            gamma_cols, shares_all, (((0,), (0,)), ((), ())), preferred_element_type=jnp.float32
        )
        latent_grad = (upstream * inverse + 2.0 * pre * back_sum).astype(jnp.bfloat16)
        lat_all = squares.shape[0]
        squares_ones = jnp.concatenate([squares, jnp.ones((128, pixels), squares.dtype)], 0)
        joined = lax.dot_general(
            shares, squares_ones, (((1,), (1,)), ((), ())), preferred_element_type=jnp.float32
        )
        scale_factor = 1.0 / math.sqrt(pixels * lax.axis_size("row"))
        if len(ring) <= 16:
            (halves,) = ring_sum([joined], ring)
            gamma_total = jnp.concatenate([h[:, :lat_all] for h in halves], 0)
            beta_total = jnp.concatenate([h[:, lat_all] for h in halves], 0)
        else:
            joined_total = lax.psum(joined, "row")
            gamma_total = joined_total[:, :lat_all]
            beta_total = joined_total[:, lat_all]
        grad_gamma = gamma_total.astype(jnp.float32) * scale_factor
        grad_beta = beta_total.astype(jnp.float32) * scale_factor
        grad_all = chan_gather(latent_grad.reshape(lat_local, row_count, col_count))
        grad_rimmed = extended(grad_all, (("row", 1),), 1)
        grad_padded = jnp.pad(grad_rimmed, ((0, 0), (0, 0), (1, 1)))
        running = jnp.zeros((in_local, pixels), jnp.float32)
        count_rows = shard_piece.shape[0]
        for tap_index, (row_shift, col_shift) in enumerate(TAPS):
            window = grad_padded[
                :, 1 - row_shift : 1 - row_shift + row_count, 1 - col_shift : 1 - col_shift + col_count
            ].reshape(count_rows, pixels)
            running = running + lax.dot_general(
                shard_piece[:, tap_index, :],
                window,
                (((0,), (0,)), ((), ())),
                preferred_element_type=jnp.float32,
            )
        return (
            latent.reshape(lat_local, row_count, col_count),
            running.reshape(in_local, row_count, col_count),
            grad_gamma,
            grad_beta,
        )

    return per_device


def solution(mesh):
    return jax.shard_map(
        make_per_device(ring_order(mesh)),
        mesh=mesh,
        in_specs=(
            P("chan", ("grp", "row"), None),
            P("row", None, "chan"),
            P("chan", None),
            P("chan"),
            P("chan", ("grp", "row"), None),
        ),
        out_specs=(
            P("chan", ("grp", "row"), None),
            P("chan", ("grp", "row"), None),
            P(("grp", "chan"), None),
            P(("grp", "chan")),
        ),
        check_vma=False,
    )
```

```python
import math

import jax
import jax.numpy as jnp
from jax import lax
from jax.sharding import PartitionSpec as P

TAPS = ((-1, -1), (-1, 0), (-1, 1), (0, -1), (0, 0), (0, 1), (1, -1), (1, 0), (1, 1))
SWAP = [(0, 1), (1, 0)]


def extended(shard, sides, width):
    for axis, dim in sides:
        count, length = (lax.axis_size(axis), shard.shape[dim])
        up = [(i, (i + 1) % count) for i in range(count - 1)]
        down = [(j, i) for i, j in up]
        last = lax.slice_in_dim(shard, length - width, length, axis=dim)
        leading = lax.slice_in_dim(shard, 0, width, axis=dim)
        before = lax.ppermute(last, axis, up)
        after = lax.ppermute(leading, axis, down)
        shard = jnp.concatenate([before, shard, after], axis=dim)
    return shard


def chan_gather(x):
    other = lax.ppermute(x, "chan", SWAP)
    both = jnp.concatenate([x, other], 0)
    return jnp.roll(both, lax.axis_index("chan") * x.shape[0], axis=0)


def chan_gather_into(mine, other):
    both = jnp.concatenate([mine, other], 0)
    return jnp.roll(both, lax.axis_index("chan") * mine.shape[0], axis=0)


def chan_scatter_sum(x):
    half = x.shape[0] // 2
    index = lax.axis_index("chan")
    mine = lax.dynamic_slice_in_dim(x, index * half, half, 0)
    theirs = lax.dynamic_slice_in_dim(x, (1 - index) * half, half, 0)
    return mine + lax.ppermute(theirs, "chan", SWAP)


def ring_order(mesh):
    count = mesh.shape["row"]
    try:
        coords = [tuple(d.coords) for d in mesh.devices[0, :, 0]]
    except Exception:
        return list(range(count))
    xs = sorted({c[0] for c in coords})
    zs = sorted({c[2] for c in coords})
    if len(xs) * len(zs) != count or len(zs) % 2:
        return list(range(count))
    where = {(c[0], c[2]): i for i, c in enumerate(coords)}
    path = [where[(xs[0], zs[0])]]
    for k, z in enumerate(zs):
        cols = xs[1:] if k % 2 == 0 else xs[:0:-1]
        path += [where[(x, z)] for x in cols]
    path += [where[(xs[0], z)] for z in zs[:0:-1]]
    return path if len(set(path)) == count else list(range(count))


def ring_sum(blocks, ring):
    count = len(ring)
    forward = [(ring[i], ring[(i + 1) % count]) for i in range(count)]
    backward = [(b, a) for a, b in forward]
    position = jnp.asarray([ring.index(i) for i in range(count)], jnp.int32)[lax.axis_index("row")]

    def chunks(x, part):
        half = x.shape[0] // 2
        piece = x[part * half : (part + 1) * half]
        return piece.reshape((count, half // count) + x.shape[1:])

    split = [[chunks(x, part) for x in blocks] for part in range(2)]
    moves = (forward, backward)
    signs = (1, -1)

    def pick(part, step):
        index = (position - signs[part] * (1 + step)) % count
        return [jnp.take(c, index, axis=0) for c in split[part]]

    carry = [pick(part, 0) for part in range(2)]
    for step in range(1, count):
        for part in range(2):
            got = lax.ppermute(carry[part], "row", moves[part])
            carry[part] = [g + o for g, o in zip(got, pick(part, step))]
    gathered = [[c.astype(jnp.bfloat16) for c in part] for part in carry]
    gathered = [[c] for c in gathered]
    for step in range(1, count):
        for part in range(2):
            gathered[part].append(lax.ppermute(gathered[part][-1], "row", moves[part]))
    results = []
    for leaf in range(len(blocks)):
        halves = []
        for part in range(2):
            stacked = jnp.stack([g[leaf] for g in gathered[part]], 0)
            order = (signs[part] * (position - jnp.arange(count))) % count
            halves.append(jnp.take(stacked, order, axis=0).reshape((-1,) + stacked.shape[2:]))
        results.append(jnp.concatenate(halves, 0).astype(jnp.float32))
    return results


def make_per_device(ring):
    def per_device(band_strip, conv_weight, gdn_gamma, gdn_beta, cotangent):
        in_local = band_strip.shape[0]
        row_count = band_strip.shape[1]
        col_count = band_strip.shape[2]
        pixels = row_count * col_count
        lat_local = gdn_gamma.shape[0]
        rimmed = extended(band_strip, (("row", 1),), 1)
        strip_padded = jnp.pad(rimmed, ((0, 0), (0, 0), (1, 1)))
        shard_piece = lax.all_gather(conv_weight, "row", axis=0, tiled=True)
        index = lax.axis_index("chan")
        windows = [
            strip_padded[
                :, 1 + row_shift : 1 + row_shift + row_count, 1 + col_shift : 1 + col_shift + col_count
            ].reshape(in_local, pixels)
            for row_shift, col_shift in TAPS
        ]

        def half_conv(start):
            rows = lax.dynamic_slice_in_dim(shard_piece, start, lat_local, 0)
            total = jnp.zeros((lat_local, pixels), jnp.float32)
            for tap_index in range(len(TAPS)):
                total = total + jnp.dot(
                    rows[:, tap_index, :], windows[tap_index], preferred_element_type=jnp.float32
                )
            return total

        sent = lax.ppermute(half_conv((1 - index) * lat_local), "chan", SWAP)
        pre = half_conv(index * lat_local) + sent
        squares_own = (pre * pre).astype(jnp.bfloat16)
        squares = chan_gather(squares_own)
        norm_value = gdn_beta[:, None] + jnp.dot(gdn_gamma, squares, preferred_element_type=jnp.float32)
        inverse = lax.rsqrt(norm_value)
        latent = (pre * inverse).astype(jnp.bfloat16)
        upstream = cotangent.reshape(lat_local, pixels).astype(jnp.float32)
        shares = (-0.5 * upstream * pre * inverse * inverse * inverse).astype(jnp.bfloat16)
        index = lax.axis_index("chan")
        gamma_mine = lax.dynamic_slice_in_dim(gdn_gamma, index * lat_local, lat_local, 1)
        gamma_theirs = lax.dynamic_slice_in_dim(gdn_gamma, (1 - index) * lat_local, lat_local, 1)
        gamma_cols = chan_gather_into(gamma_mine, lax.ppermute(gamma_theirs, "chan", SWAP))
        shares_all = chan_gather(shares)
        back_sum = lax.dot_general(
            gamma_cols, shares_all, (((0,), (0,)), ((), ())), preferred_element_type=jnp.float32
        )
        latent_grad = (upstream * inverse + 2.0 * pre * back_sum).astype(jnp.bfloat16)
        lat_all = squares.shape[0]
        squares_ones = jnp.concatenate([squares, jnp.ones((128, pixels), squares.dtype)], 0)
        joined = lax.dot_general(
            shares, squares_ones, (((1,), (1,)), ((), ())), preferred_element_type=jnp.float32
        )
        if len(ring) <= 16:
            (joined_total,) = ring_sum([joined], ring)
        else:
            joined_total = lax.psum(joined, "row")
        gamma_total = joined_total[:, :lat_all]
        beta_total = joined_total[:, lat_all]
        scale_factor = 1.0 / math.sqrt(pixels * lax.axis_size("row"))
        grad_gamma = gamma_total * scale_factor
        grad_beta = beta_total * scale_factor
        grad_all = chan_gather(latent_grad.reshape(lat_local, row_count, col_count))
        grad_rimmed = extended(grad_all, (("row", 1),), 1)
        grad_padded = jnp.pad(grad_rimmed, ((0, 0), (0, 0), (1, 1)))
        running = jnp.zeros((in_local, pixels), jnp.float32)
        count_rows = shard_piece.shape[0]
        for tap_index, (row_shift, col_shift) in enumerate(TAPS):
            window = grad_padded[
                :, 1 - row_shift : 1 - row_shift + row_count, 1 - col_shift : 1 - col_shift + col_count
            ].reshape(count_rows, pixels)
            running = running + lax.dot_general(
                shard_piece[:, tap_index, :],
                window,
                (((0,), (0,)), ((), ())),
                preferred_element_type=jnp.float32,
            )
        return (
            latent.reshape(lat_local, row_count, col_count),
            running.reshape(in_local, row_count, col_count),
            grad_gamma,
            grad_beta,
        )

    return per_device


def solution(mesh):
    return jax.shard_map(
        make_per_device(ring_order(mesh)),
        mesh=mesh,
        in_specs=(
            P("chan", ("grp", "row"), None),
            P("row", None, "chan"),
            P("chan", None),
            P("chan"),
            P("chan", ("grp", "row"), None),
        ),
        out_specs=(
            P("chan", ("grp", "row"), None),
            P("chan", ("grp", "row"), None),
            P(("grp", "chan"), None),
            P(("grp", "chan")),
        ),
        check_vma=False,
    )
```

```python
import math

import jax
import jax.numpy as jnp
from jax import lax
from jax.sharding import PartitionSpec as P

TAPS = ((-1, -1), (-1, 0), (-1, 1), (0, -1), (0, 0), (0, 1), (1, -1), (1, 0), (1, 1))
SWAP = [(0, 1), (1, 0)]


def extended(shard, sides, width):
    for axis, dim in sides:
        count, length = (lax.axis_size(axis), shard.shape[dim])
        up = [(i, (i + 1) % count) for i in range(count - 1)]
        down = [(j, i) for i, j in up]
        last = lax.slice_in_dim(shard, length - width, length, axis=dim)
        leading = lax.slice_in_dim(shard, 0, width, axis=dim)
        before = lax.ppermute(last, axis, up)
        after = lax.ppermute(leading, axis, down)
        shard = jnp.concatenate([before, shard, after], axis=dim)
    return shard


def chan_gather(x):
    other = lax.ppermute(x, "chan", SWAP)
    both = jnp.concatenate([x, other], 0)
    return jnp.roll(both, lax.axis_index("chan") * x.shape[0], axis=0)


def chan_gather_into(mine, other):
    both = jnp.concatenate([mine, other], 0)
    return jnp.roll(both, lax.axis_index("chan") * mine.shape[0], axis=0)


def chan_scatter_sum(x):
    half = x.shape[0] // 2
    index = lax.axis_index("chan")
    mine = lax.dynamic_slice_in_dim(x, index * half, half, 0)
    theirs = lax.dynamic_slice_in_dim(x, (1 - index) * half, half, 0)
    return mine + lax.ppermute(theirs, "chan", SWAP)


def ring_order(mesh):
    count = mesh.shape["row"]
    try:
        coords = [tuple(d.coords) for d in mesh.devices[0, :, 0]]
    except Exception:
        return list(range(count))
    xs = sorted({c[0] for c in coords})
    zs = sorted({c[2] for c in coords})
    if len(xs) * len(zs) != count or len(zs) % 2:
        return list(range(count))
    where = {(c[0], c[2]): i for i, c in enumerate(coords)}
    path = [where[(xs[0], zs[0])]]
    for k, z in enumerate(zs):
        cols = xs[1:] if k % 2 == 0 else xs[:0:-1]
        path += [where[(x, z)] for x in cols]
    path += [where[(xs[0], z)] for z in zs[:0:-1]]
    return path if len(set(path)) == count else list(range(count))


def ring_sum(blocks, ring):
    count = len(ring)
    forward = [(ring[i], ring[(i + 1) % count]) for i in range(count)]
    backward = [(b, a) for a, b in forward]
    position = jnp.asarray([ring.index(i) for i in range(count)], jnp.int32)[lax.axis_index("row")]

    def chunks(x, part):
        half = x.shape[0] // 2
        piece = x[part * half : (part + 1) * half]
        return piece.reshape((count, half // count) + x.shape[1:])

    split = [[chunks(x, part) for x in blocks] for part in range(2)]
    moves = (forward, backward)
    signs = (1, -1)

    def pick(part, step):
        index = (position - signs[part] * (1 + step)) % count
        return [jnp.take(c, index, axis=0) for c in split[part]]

    carry = [pick(part, 0) for part in range(2)]
    for step in range(1, count):
        for part in range(2):
            got = lax.ppermute(carry[part], "row", moves[part])
            carry[part] = [g + o for g, o in zip(got, pick(part, step))]
    gathered = [[c.astype(jnp.bfloat16) for c in part] for part in carry]
    gathered = [[c] for c in gathered]
    for step in range(1, count):
        for part in range(2):
            gathered[part].append(lax.ppermute(gathered[part][-1], "row", moves[part]))
    results = []
    for leaf in range(len(blocks)):
        halves = []
        for part in range(2):
            stacked = jnp.stack([g[leaf] for g in gathered[part]], 0)
            order = (signs[part] * (position - jnp.arange(count))) % count
            halves.append(jnp.take(stacked, order, axis=0).reshape((-1,) + stacked.shape[2:]))
        results.append(jnp.concatenate(halves, 0).astype(jnp.float32))
    return results


def make_per_device(ring):
    def per_device(band_strip, conv_weight, gdn_gamma, gdn_beta, cotangent):
        in_local = band_strip.shape[0]
        row_count = band_strip.shape[1]
        col_count = band_strip.shape[2]
        pixels = row_count * col_count
        lat_local = gdn_gamma.shape[0]
        rimmed = extended(band_strip, (("row", 1),), 1)
        strip_padded = jnp.pad(rimmed, ((0, 0), (0, 0), (1, 1)))
        shard_piece = lax.all_gather(conv_weight, "row", axis=0, tiled=True)
        index = lax.axis_index("chan")
        windows = [
            strip_padded[
                :, 1 + row_shift : 1 + row_shift + row_count, 1 + col_shift : 1 + col_shift + col_count
            ].reshape(in_local, pixels)
            for row_shift, col_shift in TAPS
        ]

        def half_conv(start):
            rows = lax.dynamic_slice_in_dim(shard_piece, start, lat_local, 0)
            total = jnp.zeros((lat_local, pixels), jnp.float32)
            for tap_index in range(len(TAPS)):
                total = total + jnp.dot(
                    rows[:, tap_index, :], windows[tap_index], preferred_element_type=jnp.float32
                )
            return total

        sent = lax.ppermute(half_conv((1 - index) * lat_local), "chan", SWAP)
        pre = half_conv(index * lat_local) + sent
        squares_own = (pre * pre).astype(jnp.bfloat16)
        squares_other = lax.ppermute(squares_own, "chan", SWAP)
        squares = jnp.roll(jnp.concatenate([squares_own, squares_other], 0), index * lat_local, axis=0)
        norm_own = jnp.dot(
            lax.dynamic_slice_in_dim(gdn_gamma, index * lat_local, lat_local, 1),
            squares_own,
            preferred_element_type=jnp.float32,
        )
        norm_other = jnp.dot(
            lax.dynamic_slice_in_dim(gdn_gamma, (1 - index) * lat_local, lat_local, 1),
            squares_other,
            preferred_element_type=jnp.float32,
        )
        norm_value = gdn_beta[:, None] + (norm_own + norm_other)
        inverse = lax.rsqrt(norm_value)
        latent = (pre * inverse).astype(jnp.bfloat16)
        upstream = cotangent.reshape(lat_local, pixels).astype(jnp.float32)
        shares = (-0.5 * upstream * pre * inverse * inverse * inverse).astype(jnp.bfloat16)
        index = lax.axis_index("chan")
        gamma_mine = lax.dynamic_slice_in_dim(gdn_gamma, index * lat_local, lat_local, 1)
        gamma_theirs = lax.dynamic_slice_in_dim(gdn_gamma, (1 - index) * lat_local, lat_local, 1)
        gamma_cols = chan_gather_into(gamma_mine, lax.ppermute(gamma_theirs, "chan", SWAP))
        shares_all = chan_gather(shares)
        back_sum = lax.dot_general(
            gamma_cols, shares_all, (((0,), (0,)), ((), ())), preferred_element_type=jnp.float32
        )
        latent_grad = (upstream * inverse + 2.0 * pre * back_sum).astype(jnp.bfloat16)
        lat_all = squares.shape[0]
        squares_ones = jnp.concatenate([squares, jnp.ones((128, pixels), squares.dtype)], 0)
        joined = lax.dot_general(
            shares, squares_ones, (((1,), (1,)), ((), ())), preferred_element_type=jnp.float32
        )
        if len(ring) <= 16:
            (joined_total,) = ring_sum([joined], ring)
        else:
            joined_total = lax.psum(joined, "row")
        gamma_total = joined_total[:, :lat_all]
        beta_total = joined_total[:, lat_all]
        scale_factor = 1.0 / math.sqrt(pixels * lax.axis_size("row"))
        grad_gamma = gamma_total * scale_factor
        grad_beta = beta_total * scale_factor
        grad_all = chan_gather(latent_grad.reshape(lat_local, row_count, col_count))
        grad_rimmed = extended(grad_all, (("row", 1),), 1)
        grad_padded = jnp.pad(grad_rimmed, ((0, 0), (0, 0), (1, 1)))
        running = jnp.zeros((in_local, pixels), jnp.float32)
        count_rows = shard_piece.shape[0]
        for tap_index, (row_shift, col_shift) in enumerate(TAPS):
            window = grad_padded[
                :, 1 - row_shift : 1 - row_shift + row_count, 1 - col_shift : 1 - col_shift + col_count
            ].reshape(count_rows, pixels)
            running = running + lax.dot_general(
                shard_piece[:, tap_index, :],
                window,
                (((0,), (0,)), ((), ())),
                preferred_element_type=jnp.float32,
            )
        return (
            latent.reshape(lat_local, row_count, col_count),
            running.reshape(in_local, row_count, col_count),
            grad_gamma,
            grad_beta,
        )

    return per_device


def solution(mesh):
    return jax.shard_map(
        make_per_device(ring_order(mesh)),
        mesh=mesh,
        in_specs=(
            P("chan", ("grp", "row"), None),
            P("row", None, "chan"),
            P("chan", None),
            P("chan"),
            P("chan", ("grp", "row"), None),
        ),
        out_specs=(
            P("chan", ("grp", "row"), None),
            P("chan", ("grp", "row"), None),
            P(("grp", "chan"), None),
            P(("grp", "chan")),
        ),
        check_vma=False,
    )
```

```python
import math

import jax
import jax.numpy as jnp
from jax import lax
from jax.sharding import PartitionSpec as P

TAPS = ((-1, -1), (-1, 0), (-1, 1), (0, -1), (0, 0), (0, 1), (1, -1), (1, 0), (1, 1))
SWAP = [(0, 1), (1, 0)]


def extended(shard, sides, width):
    for axis, dim in sides:
        count, length = (lax.axis_size(axis), shard.shape[dim])
        up = [(i, (i + 1) % count) for i in range(count - 1)]
        down = [(j, i) for i, j in up]
        last = lax.slice_in_dim(shard, length - width, length, axis=dim)
        leading = lax.slice_in_dim(shard, 0, width, axis=dim)
        before = lax.ppermute(last, axis, up)
        after = lax.ppermute(leading, axis, down)
        shard = jnp.concatenate([before, shard, after], axis=dim)
    return shard


def chan_gather(x):
    other = lax.ppermute(x, "chan", SWAP)
    both = jnp.concatenate([x, other], 0)
    return jnp.roll(both, lax.axis_index("chan") * x.shape[0], axis=0)


def chan_gather_into(mine, other):
    both = jnp.concatenate([mine, other], 0)
    return jnp.roll(both, lax.axis_index("chan") * mine.shape[0], axis=0)


def chan_scatter_sum(x):
    half = x.shape[0] // 2
    index = lax.axis_index("chan")
    mine = lax.dynamic_slice_in_dim(x, index * half, half, 0)
    theirs = lax.dynamic_slice_in_dim(x, (1 - index) * half, half, 0)
    return mine + lax.ppermute(theirs, "chan", SWAP)


def ring_order(mesh):
    count = mesh.shape["row"]
    try:
        coords = [tuple(d.coords) for d in mesh.devices[0, :, 0]]
    except Exception:
        return list(range(count))
    xs = sorted({c[0] for c in coords})
    zs = sorted({c[2] for c in coords})
    if len(xs) * len(zs) != count or len(zs) % 2:
        return list(range(count))
    where = {(c[0], c[2]): i for i, c in enumerate(coords)}
    path = [where[(xs[0], zs[0])]]
    for k, z in enumerate(zs):
        cols = xs[1:] if k % 2 == 0 else xs[:0:-1]
        path += [where[(x, z)] for x in cols]
    path += [where[(xs[0], z)] for z in zs[:0:-1]]
    return path if len(set(path)) == count else list(range(count))


def ring_sum(blocks, ring):
    count = len(ring)
    forward = [(ring[i], ring[(i + 1) % count]) for i in range(count)]
    backward = [(b, a) for a, b in forward]
    position = jnp.asarray([ring.index(i) for i in range(count)], jnp.int32)[lax.axis_index("row")]

    def chunks(x, part):
        half = x.shape[0] // 2
        piece = x[part * half : (part + 1) * half]
        return piece.reshape((count, half // count) + x.shape[1:])

    split = [[chunks(x, part) for x in blocks] for part in range(2)]
    moves = (forward, backward)
    signs = (1, -1)

    def pick(part, step):
        index = (position - signs[part] * (1 + step)) % count
        return [jnp.take(c, index, axis=0) for c in split[part]]

    carry = [pick(part, 0) for part in range(2)]
    for step in range(1, count):
        for part in range(2):
            got = lax.ppermute(carry[part], "row", moves[part])
            carry[part] = [g + o for g, o in zip(got, pick(part, step))]
    gathered = [[c.astype(jnp.bfloat16) for c in part] for part in carry]
    gathered = [[c] for c in gathered]
    for step in range(1, count):
        for part in range(2):
            gathered[part].append(lax.ppermute(gathered[part][-1], "row", moves[part]))
    results = []
    for leaf in range(len(blocks)):
        halves = []
        for part in range(2):
            stacked = jnp.stack([g[leaf] for g in gathered[part]], 0)
            order = (signs[part] * (position - jnp.arange(count))) % count
            halves.append(jnp.take(stacked, order, axis=0).reshape((-1,) + stacked.shape[2:]))
        results.append(jnp.concatenate(halves, 0).astype(jnp.float32))
    return results


def make_per_device(ring):
    def per_device(band_strip, conv_weight, gdn_gamma, gdn_beta, cotangent):
        in_local = band_strip.shape[0]
        row_count = band_strip.shape[1]
        col_count = band_strip.shape[2]
        pixels = row_count * col_count
        lat_local = gdn_gamma.shape[0]
        rimmed = extended(band_strip, (("row", 1),), 1)
        strip_padded = jnp.pad(rimmed, ((0, 0), (0, 0), (1, 1)))
        shard_piece = lax.all_gather(conv_weight, "row", axis=0, tiled=True)
        index = lax.axis_index("chan")
        windows = [
            strip_padded[
                :, 1 + row_shift : 1 + row_shift + row_count, 1 + col_shift : 1 + col_shift + col_count
            ].reshape(in_local, pixels)
            for row_shift, col_shift in TAPS
        ]

        def half_conv(start, size=lat_local):
            rows = lax.dynamic_slice_in_dim(shard_piece, start, size, 0)
            total = jnp.zeros((size, pixels), jnp.float32)
            for tap_index in range(len(TAPS)):
                total = total + jnp.dot(
                    rows[:, tap_index, :], windows[tap_index], preferred_element_type=jnp.float32
                )
            return total

        quarter = lat_local // 2
        sent = jnp.concatenate(
            [
                lax.ppermute(half_conv((1 - index) * lat_local + k * quarter, quarter), "chan", SWAP)
                for k in range(2)
            ],
            0,
        )
        pre = half_conv(index * lat_local) + sent
        squares_own = (pre * pre).astype(jnp.bfloat16)
        squares = chan_gather(squares_own)
        norm_value = gdn_beta[:, None] + jnp.dot(gdn_gamma, squares, preferred_element_type=jnp.float32)
        inverse = lax.rsqrt(norm_value)
        latent = (pre * inverse).astype(jnp.bfloat16)
        upstream = cotangent.reshape(lat_local, pixels).astype(jnp.float32)
        shares = (-0.5 * upstream * pre * inverse * inverse * inverse).astype(jnp.bfloat16)
        index = lax.axis_index("chan")
        gamma_mine = lax.dynamic_slice_in_dim(gdn_gamma, index * lat_local, lat_local, 1)
        gamma_theirs = lax.dynamic_slice_in_dim(gdn_gamma, (1 - index) * lat_local, lat_local, 1)
        gamma_cols = chan_gather_into(gamma_mine, lax.ppermute(gamma_theirs, "chan", SWAP))
        shares_all = chan_gather(shares)
        back_sum = lax.dot_general(
            gamma_cols, shares_all, (((0,), (0,)), ((), ())), preferred_element_type=jnp.float32
        )
        latent_grad = (upstream * inverse + 2.0 * pre * back_sum).astype(jnp.bfloat16)
        lat_all = squares.shape[0]
        squares_ones = jnp.concatenate([squares, jnp.ones((128, pixels), squares.dtype)], 0)
        joined = lax.dot_general(
            shares, squares_ones, (((1,), (1,)), ((), ())), preferred_element_type=jnp.float32
        )
        if len(ring) <= 16:
            (joined_total,) = ring_sum([joined], ring)
        else:
            joined_total = lax.psum(joined, "row")
        gamma_total = joined_total[:, :lat_all]
        beta_total = joined_total[:, lat_all]
        scale_factor = 1.0 / math.sqrt(pixels * lax.axis_size("row"))
        grad_gamma = gamma_total * scale_factor
        grad_beta = beta_total * scale_factor
        grad_all = chan_gather(latent_grad.reshape(lat_local, row_count, col_count))
        grad_rimmed = extended(grad_all, (("row", 1),), 1)
        grad_padded = jnp.pad(grad_rimmed, ((0, 0), (0, 0), (1, 1)))
        running = jnp.zeros((in_local, pixels), jnp.float32)
        count_rows = shard_piece.shape[0]
        for tap_index, (row_shift, col_shift) in enumerate(TAPS):
            window = grad_padded[
                :, 1 - row_shift : 1 - row_shift + row_count, 1 - col_shift : 1 - col_shift + col_count
            ].reshape(count_rows, pixels)
            running = running + lax.dot_general(
                shard_piece[:, tap_index, :],
                window,
                (((0,), (0,)), ((), ())),
                preferred_element_type=jnp.float32,
            )
        return (
            latent.reshape(lat_local, row_count, col_count),
            running.reshape(in_local, row_count, col_count),
            grad_gamma,
            grad_beta,
        )

    return per_device


def solution(mesh):
    return jax.shard_map(
        make_per_device(ring_order(mesh)),
        mesh=mesh,
        in_specs=(
            P("chan", ("grp", "row"), None),
            P("row", None, "chan"),
            P("chan", None),
            P("chan"),
            P("chan", ("grp", "row"), None),
        ),
        out_specs=(
            P("chan", ("grp", "row"), None),
            P("chan", ("grp", "row"), None),
            P(("grp", "chan"), None),
            P(("grp", "chan")),
        ),
        check_vma=False,
    )
```
